32 devices in a mesh: line: 16 (over z, y, x), chan: 2 (over core).
Axes of the slice: x: 2, y: 2, z: 4, core: 2. Of those that a mesh axis runs over, the one named last changes fastest.
Arguments:
- observed: float32 [2, 16, 128, 16384], P(None, 'chan', None, 'line'), may hold values from -6 to 6
- current_image: float32 [2, 16, 128, 16384], P(None, 'chan', 'line'), may hold values from -4 to 4
- previous_image: float32 [2, 16, 128, 16384], P(None, 'chan', 'line'), may hold values from -4 to 4
- doppler_phase: float32 [128, 16384], P(None, 'line'), may hold values from -3.140625 to 3.140625
- channel_ramp: float32 [16, 16384], P('chan', 'line'), may hold values from -3.140625 to 3.140625
- range_offset: int32 [16384], P('line'), may hold values from -2 to 2
- tap_index: int32 [16384], P('line'), may hold values from 0 to 15
- kernel_table: float32 [16, 4], replicated, may hold values from -0.5 to 0.5
- group_of: int32 [16], P('chan'), may hold values from 0 to 3
- calib_gain: float32 [4], replicated, may hold values from 0.5 to 2
Outputs:
- next_image: float32 [2, 16, 128, 16384], P(None, 'chan', 'line')
- prior_image: float32 [2, 16, 128, 16384], P(None, 'chan', 'line')
The draws below stay inside these ranges and needn't reach their ends.
All inputs are finite; a program needn't handle non-finite values.
Results may differ from the reference program's by a relative error of at most 0.0003.
Values sent between devices are 32-bit elements; how exact they have to be, the bound alone decides.
No kernel may reach another device: no remote copies, remote signals or barrier semaphores. Data moves between devices by JAX's collectives and lax.ppermute only.
A program may use at most 192 MiB of HBM per device.

```python
import math
import jax
import jax.numpy as jnp
from jax import lax

C = 16
NA = 16384
RG = 128
K = 4
Q = 16
OFFMAX = 2
G = 4
ITERS = 2
START_ITER = 8


def set_ends(array, key, low, high):
    longest = array.shape.index(max(array.shape))
    spots = []
    for shift in (0, 1):
        where = [jax.random.randint(jax.random.fold_in(key, axis), (), 0, length) for axis, length in enumerate(array.shape)]
        where[longest] = (where[longest] + shift) % array.shape[longest]
        spots.append(tuple(where))
    return array.at[spots[0]].set(low).at[spots[1]].set(high)


def level_of(own_key, shape, cuts, least, top_value):
    def one(dim, parts):
        draws = jax.random.uniform(jax.random.fold_in(jax.random.fold_in(own_key, 6), dim), (parts,), jnp.float32, least / len(cuts), top_value / len(cuts))
        return jnp.repeat(jnp.exp(draws), shape[dim] // parts).reshape((-1,) + (1,) * (len(shape) - dim - 1))

    loudness = one(*cuts[0])
    for cut in cuts[1:]:
        loudness = loudness * one(*cut)
    return loudness


def gaussian(own_key, dims, scale, most, pieces=(), held_as=jnp.bfloat16):
    loudness = level_of(own_key, dims, pieces, -0.22, 0.18) if pieces else 1.0
    drawn = jax.random.normal(own_key, dims, jnp.float32) * scale * loudness
    return jnp.minimum(jnp.maximum(drawn, -most), most).astype(held_as)


def setup_inputs(seed: int = 0) -> dict:
    key_of = jax.random.split(jax.random.key(seed), 11)
    observed = gaussian(key_of[0], (2, C, RG, NA), 1.0, 6.0, ((1, 2), (3, 16)), jnp.float32)
    current_image = gaussian(key_of[1], (2, C, RG, NA), 0.5, 4.0, ((1, 2), (2, 16)), jnp.float32)
    previous_image = gaussian(key_of[2], (2, C, RG, NA), 0.5, 4.0, ((1, 2), (2, 16)), jnp.float32)
    doppler_phase = jnp.clip(jax.random.uniform(key_of[3], (RG, NA), jnp.float32, -3.140625, 3.140625), -3.140625, 3.140625)
    channel_ramp = jnp.clip(jax.random.uniform(key_of[4], (C, NA), jnp.float32, -3.140625, 3.140625), -3.140625, 3.140625)
    range_offset = set_ends(jax.random.randint(key_of[5], (NA,), 0 - OFFMAX, OFFMAX + 1), jax.random.fold_in(key_of[5], 1), 0 - OFFMAX, OFFMAX).astype(jnp.int32)
    tap_index = set_ends(jax.random.randint(key_of[6], (NA,), 0, Q), jax.random.fold_in(key_of[6], 1), 0, Q - 1).astype(jnp.int32)
    kernel_table = jnp.clip(jax.random.uniform(key_of[7], (Q, K), jnp.float32, -0.5, 0.5), -0.5, 0.5)
    group_of = set_ends(jax.random.randint(key_of[8], (C,), 0, G), jax.random.fold_in(key_of[8], 1), 0, G - 1).astype(jnp.int32)
    calib_gain = jnp.clip(jnp.exp(jax.random.uniform(key_of[9], (G,), jnp.float32, math.log(0.5), math.log(2.0))), 0.5, 2.0)
    return {"observed": observed, "current_image": current_image, "previous_image": previous_image, "doppler_phase": doppler_phase, "channel_ramp": channel_ramp, "range_offset": range_offset, "tap_index": tap_index, "kernel_table": kernel_table, "group_of": group_of, "calib_gain": calib_gain}


step_length = 0.25
threshold = 3.0

def momentum_weights():
    current = 1.0
    for counter in range(1, START_ITER):
        current = (1.0 + math.sqrt(1.0 + 4.0 * current * current)) / 2.0
    momenta = []
    for counter in range(ITERS):
        following = (1.0 + math.sqrt(1.0 + 4.0 * current * current)) / 2.0
        momenta.append((current - 1.0) / following)
        current = following
    return momenta

def shift_weights(range_offset, tap_index, kernel_table):
    levels = jnp.arange(Q, dtype=jnp.int32)
    onehot = (tap_index[:, None] == levels[None, :]).astype(jnp.float32)
    tap_weights = jnp.dot(onehot, kernel_table, precision=lax.Precision.HIGHEST, preferred_element_type=jnp.float32)
    stacked = []
    for displacement in range(-(OFFMAX + K // 2 - 1), OFFMAX + K // 2 + 1):
        summed = jnp.zeros(range_offset.shape, jnp.float32)
        for tap_number in range(K):
            matches = (range_offset + (tap_number - (K // 2 - 1)) == displacement).astype(jnp.float32)
            summed = summed + tap_weights[:, tap_number] * matches
        stacked.append(summed)
    return jnp.stack(stacked)

def shifted_sum(padded, weights, row_count, adjoint):
    rim_width = OFFMAX + K // 2
    lowest = -(OFFMAX + K // 2 - 1)
    summed = None
    for position in range(weights.shape[0]):
        displacement = lowest + position
        anchor = rim_width - displacement if adjoint else rim_width + displacement
        sliced = lax.slice_in_dim(padded, anchor, anchor + row_count, axis=padded.ndim - 2)
        weighted = sliced * weights[position]
        summed = weighted if summed is None else summed + weighted
    return summed

def reference(observed, current_image, previous_image, doppler_phase, channel_ramp, range_offset, tap_index, kernel_table, group_of, calib_gain):
    rim_width = OFFMAX + K // 2
    weights = shift_weights(range_offset, tap_index, kernel_table)
    channel_gain = calib_gain[group_of]
    measured = jnp.moveaxis(observed, 1, 0)
    momenta = momentum_weights()
    earlier = previous_image
    latest = current_image
    for iteration in range(ITERS):
        blended = latest + momenta[iteration] * (latest - earlier)

        def descend(inputs):
            latent, target, ramp_row, gain_value = inputs
            spectrum = jnp.fft.fft(latent[0] + 1j * latent[1], axis=-1, norm='ortho')
            padded = jnp.pad(spectrum, ((rim_width, rim_width), (0, 0)))
            migrated = shifted_sum(padded, weights, RG, False)
            phasor = gain_value * jnp.exp(1j * (doppler_phase + ramp_row[None, :]))
            misfit = phasor * migrated - (target[0] + 1j * target[1])
            returned = jnp.conj(phasor) * misfit
            spread = shifted_sum(jnp.pad(returned, ((rim_width, rim_width), (0, 0))), weights, RG, True)
            gradient = jnp.fft.ifft(spread, axis=-1, norm='ortho')
            return latent - step_length * jnp.stack([jnp.real(gradient), jnp.imag(gradient)])
        shifted = lax.map(descend, (jnp.moveaxis(blended, 1, 0), measured, channel_ramp, channel_gain))
        shifted = jnp.moveaxis(shifted, 0, 1)
        magnitude = jnp.sqrt(lax.optimization_barrier(jnp.sum(shifted * shifted, axis=(0, 1))))
        factor = jnp.maximum(magnitude - threshold, 0.0) / jnp.maximum(magnitude, threshold)
        earlier = latest
        latest = shifted * factor[None, None]
    return (latest, earlier)
```

```python
import math

import numpy as np
import jax
import jax.numpy as jnp
from jax import lax
from jax.sharding import PartitionSpec as P

K = 4
Q = 16
OFFMAX = 2
G = 4
ITERS = 2
START_ITER = 8
HALO = K - 1

step_length = 0.25
threshold = 3.0


def momentum_weights():
    current = 1.0
    for counter in range(1, START_ITER):
        current = (1.0 + math.sqrt(1.0 + 4.0 * current * current)) / 2.0
    momenta = []
    for counter in range(ITERS):
        following = (1.0 + math.sqrt(1.0 + 4.0 * current * current)) / 2.0
        momenta.append((current - 1.0) / following)
        current = following
    return momenta


def tap_table(tap_index, kernel_table):
    levels = jnp.arange(Q, dtype=jnp.int32)
    onehot = (tap_index[:, None] == levels[None, :]).astype(jnp.float32)
    return jnp.dot(
        onehot, kernel_table, precision=lax.Precision.HIGHEST, preferred_element_type=jnp.float32
    )


def shift_weights(range_offset, tap_weights):
    stacked = []
    for displacement in range(-(OFFMAX + K // 2 - 1), OFFMAX + K // 2 + 1):
        summed = jnp.zeros(range_offset.shape, jnp.float32)
        for tap_number in range(K):
            matches = (range_offset + (tap_number - (K // 2 - 1)) == displacement).astype(
                jnp.float32
            )
            summed = summed + tap_weights[..., tap_number] * matches
        stacked.append(summed)
    return jnp.stack(stacked)


LOWEST = -(OFFMAX + K // 2 - 1)


def adjoint_shift(rows, weights):
    rim_width = OFFMAX + K // 2
    count = rows.shape[-2]
    pad = [(0, 0)] * rows.ndim
    pad[-2] = (rim_width, rim_width)
    padded = jnp.pad(rows, pad)
    summed = None
    for position in range(weights.shape[0]):
        displacement = LOWEST + position
        anchor = rim_width - displacement
        sliced = lax.slice_in_dim(padded, anchor, anchor + count, axis=rows.ndim - 2)
        weighted = sliced * weights[position]
        summed = weighted if summed is None else summed + weighted
    return summed


def dft_matrix(count, sign, scale):
    counter = np.arange(count)
    angle = (np.outer(counter, counter) % count) * (2.0 * np.pi / count)
    return (
        jnp.asarray(np.cos(angle) * scale, jnp.float32),
        jnp.asarray(sign * np.sin(angle) * scale, jnp.float32),
    )


def twiddle(rows, cols, total, sign):
    angle = (np.outer(np.arange(rows), np.arange(cols)) % total) * (2.0 * np.pi / total)
    return jnp.asarray(np.cos(angle), jnp.float32), jnp.asarray(sign * np.sin(angle), jnp.float32)


def mm(pattern, a, b):
    return jnp.einsum(
        pattern, a, b, precision=lax.Precision.HIGHEST, preferred_element_type=jnp.float32
    )


def forward_transform(xr, xi, p_len, q_len):
    wc, ws = dft_matrix(p_len, -1.0, 1.0)
    vc, vs = dft_matrix(q_len, -1.0, 1.0)
    tc, ts = twiddle(p_len, q_len, p_len * q_len, -1.0)
    mr = mm("kp,bpq->bkq", wc, xr) - mm("kp,bpq->bkq", ws, xi)
    mi = mm("kp,bpq->bkq", wc, xi) + mm("kp,bpq->bkq", ws, xr)
    tr = mr * tc - mi * ts
    ti = mi * tc + mr * ts
    out_r = mm("bkq,qj->bkj", tr, vc) - mm("bkq,qj->bkj", ti, vs)
    out_i = mm("bkq,qj->bkj", ti, vc) + mm("bkq,qj->bkj", tr, vs)
    return out_r, out_i


def inverse_transform(yr, yi, p_len, q_len):
    wc, ws = dft_matrix(p_len, 1.0, 1.0)
    vc, vs = dft_matrix(q_len, 1.0, 1.0)
    tc, ts = twiddle(p_len, q_len, p_len * q_len, 1.0)
    mr = mm("bkj,jq->bkq", yr, vc) - mm("bkj,jq->bkq", yi, vs)
    mi = mm("bkj,jq->bkq", yi, vc) + mm("bkj,jq->bkq", yr, vs)
    tr = mr * tc - mi * ts
    ti = mi * tc + mr * ts
    out_r = mm("pk,bkq->bpq", wc, tr) - mm("pk,bkq->bpq", ws, ti)
    out_i = mm("pk,bkq->bpq", wc, ti) + mm("pk,bkq->bpq", ws, tr)
    return out_r, out_i


def shrink(squares):
    magnitude = jnp.sqrt(squares)
    return jnp.maximum(magnitude - threshold, 0.0) / jnp.maximum(magnitude, threshold)


def body(
    observed,
    current_image,
    previous_image,
    doppler_phase,
    channel_ramp,
    range_offset,
    tap_index,
    kernel_table,
    group_of,
    calib_gain,
):
    lines = lax.axis_size("line")
    chans = lax.axis_size("chan")
    me = lax.axis_index("line")
    _, cl, rows, na = current_image.shape
    p_len = 128 if na % 128 == 0 else 1
    q_len = na // p_len

    levels = jnp.arange(G, dtype=jnp.int32)
    channel_gain = jnp.sum(
        (group_of[:, None] == levels[None, :]).astype(jnp.float32) * calib_gain[None, :], axis=1
    )

    local_taps = tap_table(tap_index, kernel_table)
    local_weights = shift_weights(range_offset, local_taps)
    angles = doppler_phase[None, :, :] + channel_ramp[:, None, :]
    cos_a = jnp.cos(angles)
    sin_a = jnp.sin(angles)
    gain = channel_gain[:, None, None]
    back_r = gain * (cos_a * observed[0] + sin_a * observed[1])
    back_i = gain * (cos_a * observed[1] - sin_a * observed[0])
    data = adjoint_shift(jnp.stack([back_r, back_i]), local_weights)
    data = data * (step_length / math.sqrt(na))
    data = lax.all_to_all(data, "line", split_axis=2, concat_axis=3, tiled=True)
    data = data.reshape(2, cl, rows, q_len, p_len).swapaxes(-1, -2)

    packed = lax.all_gather(jnp.stack([tap_index, range_offset]), "line", axis=1, tiled=True)
    taps = tap_table(packed[0], kernel_table)
    weights = shift_weights(packed[1], taps)

    def spectral(v):
        return v.reshape(v.shape[:-1] + (q_len, p_len)).swapaxes(-1, -2)

    weights = spectral(weights)
    band = [
        spectral(sum(taps[:, k] * taps[:, k + e] for k in range(K - e))) for e in range(K)
    ]
    coef = (channel_gain * channel_gain) * (step_length / na)

    momenta = momentum_weights()
    earlier = previous_image
    latest = current_image
    forward_pairs = [(i, i + 1) for i in range(lines - 1)]
    backward_pairs = [(i + 1, i) for i in range(lines - 1)]
    first = (me == 0)
    last = (me == lines - 1)

    def wgt(d):
        return weights[d - LOWEST]

    for iteration in range(ITERS):
        blended = latest + momenta[iteration] * (latest - earlier)
        low = lax.ppermute(blended[:, :, rows - HALO :], "line", forward_pairs)
        high = lax.ppermute(blended[:, :, :HALO], "line", backward_pairs)
        ext = jnp.concatenate([low, blended, high], axis=2)
        ext_rows = rows + 2 * HALO
        xr, xi = forward_transform(
            ext[0].reshape(-1, p_len, q_len), ext[1].reshape(-1, p_len, q_len), p_len, q_len
        )
        spec = jnp.stack([xr, xi]).reshape(2, cl, ext_rows, p_len, q_len)

        def at(r):
            return spec[:, :, r]

        gram = []
        for r in range(rows):
            c = r + HALO
            acc = band[0] * at(c)
            for e in range(1, K):
                acc = acc + band[e] * (at(c - e) + at(c + e))
            gram.append(acc)
        low_fix = []
        for rr in range(K):
            acc = None
            for s in range(1, K + 1):
                if rr + s > OFFMAX + K // 2:
                    continue
                u = None
                for j in range(K):
                    if j + s > OFFMAX + K // 2:
                        continue
                    term = wgt(j + s) * at(HALO + j)
                    u = term if u is None else u + term
                term = wgt(rr + s) * u
                acc = term if acc is None else acc + term
            low_fix.append(acc)
        high_fix = []
        for tt in range(-(K - 2), 1):
            acc = None
            for s in range(1, K):
                if tt - s < LOWEST:
                    continue
                u = None
                for t in range(-(K - 2), 1):
                    if t - s < LOWEST:
                        continue
                    term = wgt(t - s) * at(HALO + rows - 1 + t)
                    u = term if u is None else u + term
                term = wgt(tt - s) * u
                acc = term if acc is None else acc + term
            high_fix.append(acc)
        for rr in range(K):
            gram[rr] = gram[rr] - jnp.where(first, low_fix[rr], 0.0)
        for idx, tt in enumerate(range(-(K - 2), 1)):
            r = rows - 1 + tt
            gram[r] = gram[r] - jnp.where(last, high_fix[idx], 0.0)
        gram = jnp.stack(gram, axis=2)
        resid = coef[None, :, None, None, None] * gram - data
        gr, gi = inverse_transform(
            resid[0].reshape(-1, p_len, q_len), resid[1].reshape(-1, p_len, q_len), p_len, q_len
        )
        shifted = blended - jnp.stack([gr, gi]).reshape(blended.shape)
        squares = jnp.sum(shifted * shifted, axis=(0, 1))
        if chans == 2:
            squares = squares + lax.ppermute(squares, "chan", [(0, 1), (1, 0)])
        else:
            squares = lax.psum(squares, "chan")
        factor = shrink(squares)
        earlier = latest
        latest = shifted * factor[None, None]
    return (latest, earlier)


def solution(mesh):
    in_specs = (
        P(None, "chan", None, "line"),
        P(None, "chan", "line", None),
        P(None, "chan", "line", None),
        P(None, "line"),
        P("chan", "line"),
        P("line"),
        P("line"),
        P(),
        P("chan"),
        P(),
    )
    out_specs = (P(None, "chan", "line", None), P(None, "chan", "line", None))
    return jax.shard_map(body, mesh=mesh, in_specs=in_specs, out_specs=out_specs, check_vma=False)
```

```python
import math

import numpy as np
import jax
import jax.numpy as jnp
from jax import lax
from jax.sharding import PartitionSpec as P
from jax.experimental import pallas as pl

K = 4
Q = 16
OFFMAX = 2
G = 4
ITERS = 2
START_ITER = 8
HALO = K - 1

step_length = 0.25
threshold = 3.0


def momentum_weights():
    current = 1.0
    for counter in range(1, START_ITER):
        current = (1.0 + math.sqrt(1.0 + 4.0 * current * current)) / 2.0
    momenta = []
    for counter in range(ITERS):
        following = (1.0 + math.sqrt(1.0 + 4.0 * current * current)) / 2.0
        momenta.append((current - 1.0) / following)
        current = following
    return momenta


def tap_table(tap_index, kernel_table):
    levels = jnp.arange(Q, dtype=jnp.int32)
    onehot = (tap_index[:, None] == levels[None, :]).astype(jnp.float32)
    return jnp.dot(
        onehot, kernel_table, precision=lax.Precision.HIGHEST, preferred_element_type=jnp.float32
    )


def shift_weights(range_offset, tap_weights):
    stacked = []
    for displacement in range(-(OFFMAX + K // 2 - 1), OFFMAX + K // 2 + 1):
        summed = jnp.zeros(range_offset.shape, jnp.float32)
        for tap_number in range(K):
            matches = (range_offset + (tap_number - (K // 2 - 1)) == displacement).astype(
                jnp.float32
            )
            summed = summed + tap_weights[..., tap_number] * matches
        stacked.append(summed)
    return jnp.stack(stacked)


LOWEST = -(OFFMAX + K // 2 - 1)


def adjoint_shift(rows, weights):
    rim_width = OFFMAX + K // 2
    count = rows.shape[-2]
    pad = [(0, 0)] * rows.ndim
    pad[-2] = (rim_width, rim_width)
    padded = jnp.pad(rows, pad)
    summed = None
    for position in range(weights.shape[0]):
        displacement = LOWEST + position
        anchor = rim_width - displacement
        sliced = lax.slice_in_dim(padded, anchor, anchor + count, axis=rows.ndim - 2)
        weighted = sliced * weights[position]
        summed = weighted if summed is None else summed + weighted
    return summed


def left_block(count, sign):
    counter = np.arange(count)
    angle = (np.outer(counter, counter) % count) * (2.0 * np.pi / count)
    c = np.cos(angle)
    s = sign * np.sin(angle)
    return jnp.asarray(np.block([[c, -s], [s, c]]), jnp.float32)


def right_block(count, sign):
    counter = np.arange(count)
    angle = (np.outer(counter, counter) % count) * (2.0 * np.pi / count)
    c = np.cos(angle)
    s = sign * np.sin(angle)
    return jnp.asarray(np.block([[c, s], [-s, c]]), jnp.float32)


def twiddle(rows, cols, total, sign):
    angle = (np.outer(np.arange(rows), np.arange(cols)) % total) * (2.0 * np.pi / total)
    return jnp.asarray(np.stack([np.cos(angle), sign * np.sin(angle)]), jnp.float32)


def dot(a, b):
    return jnp.dot(a, b, precision=lax.Precision.HIGHEST, preferred_element_type=jnp.float32)


def forward_kernel(x_ref, w_ref, v_ref, t_ref, o_ref):
    nb, p_len, q_len = x_ref.shape[1], x_ref.shape[2], x_ref.shape[3]
    stacked = jnp.concatenate(
        [
            jnp.concatenate([x_ref[0, b] for b in range(nb)], axis=1),
            jnp.concatenate([x_ref[1, b] for b in range(nb)], axis=1),
        ],
        axis=0,
    )
    mid = dot(w_ref[...], stacked)
    tc = jnp.concatenate([t_ref[0]] * nb, axis=1)
    ts = jnp.concatenate([t_ref[1]] * nb, axis=1)
    mr = mid[:p_len]
    mi = mid[p_len:]
    tr = mr * tc - mi * ts
    ti = mi * tc + mr * ts
    turned = jnp.concatenate(
        [
            jnp.concatenate([tr[:, b * q_len : (b + 1) * q_len], ti[:, b * q_len : (b + 1) * q_len]], axis=1)
            for b in range(nb)
        ],
        axis=0,
    )
    out = dot(turned, v_ref[...])
    for b in range(nb):
        o_ref[0, b] = out[b * p_len : (b + 1) * p_len, :q_len]
        o_ref[1, b] = out[b * p_len : (b + 1) * p_len, q_len:]


def inverse_kernel(y_ref, v_ref, w_ref, t_ref, o_ref):
    nb, p_len, q_len = y_ref.shape[1], y_ref.shape[2], y_ref.shape[3]
    stacked = jnp.concatenate(
        [jnp.concatenate([y_ref[0, b], y_ref[1, b]], axis=1) for b in range(nb)], axis=0
    )
    mid = dot(stacked, v_ref[...])
    tc = jnp.concatenate([t_ref[0]] * nb, axis=0)
    ts = jnp.concatenate([t_ref[1]] * nb, axis=0)
    mr = mid[:, :q_len]
    mi = mid[:, q_len:]
    tr = mr * tc - mi * ts
    ti = mi * tc + mr * ts
    turned = jnp.concatenate(
        [
            jnp.concatenate([tr[b * p_len : (b + 1) * p_len] for b in range(nb)], axis=1),
            jnp.concatenate([ti[b * p_len : (b + 1) * p_len] for b in range(nb)], axis=1),
        ],
        axis=0,
    )
    out = dot(w_ref[...], turned)
    for b in range(nb):
        o_ref[0, b] = out[:p_len, b * q_len : (b + 1) * q_len]
        o_ref[1, b] = out[p_len:, b * q_len : (b + 1) * q_len]


def block_count(total):
    for nb in (8, 7, 6, 5, 4, 3, 2, 1):
        if total % nb == 0:
            return nb
    return 1


def run_transform(kernel, data, first, second, turn):
    _, total, p_len, q_len = data.shape
    nb = block_count(total)
    flops = 2 * 2 * total * (2 * p_len) * (2 * q_len) * (p_len + q_len) // 2
    return pl.pallas_call(
        kernel,
        out_shape=jax.ShapeDtypeStruct(data.shape, jnp.float32),
        grid=(total // nb,),
        in_specs=[
            pl.BlockSpec((2, nb, p_len, q_len), lambda i: (0, i, 0, 0)),
            pl.BlockSpec(first.shape, lambda i: (0, 0)),
            pl.BlockSpec(second.shape, lambda i: (0, 0)),
            pl.BlockSpec(turn.shape, lambda i: (0, 0, 0)),
        ],
        out_specs=pl.BlockSpec((2, nb, p_len, q_len), lambda i: (0, i, 0, 0)),
        cost_estimate=pl.CostEstimate(
            flops=flops, bytes_accessed=2 * data.size * 4, transcendentals=0
        ),
    )(data, first, second, turn)


def forward_transform(x, p_len, q_len):
    return run_transform(
        forward_kernel,
        x,
        left_block(p_len, -1.0),
        right_block(q_len, -1.0),
        twiddle(p_len, q_len, p_len * q_len, -1.0),
    )


def inverse_transform(y, p_len, q_len):
    return run_transform(
        inverse_kernel,
        y,
        right_block(q_len, 1.0),
        left_block(p_len, 1.0),
        twiddle(p_len, q_len, p_len * q_len, 1.0),
    )


def shrink(squares):
    magnitude = jnp.sqrt(squares)
    return jnp.maximum(magnitude - threshold, 0.0) / jnp.maximum(magnitude, threshold)


def body(
    observed,
    current_image,
    previous_image,
    doppler_phase,
    channel_ramp,
    range_offset,
    tap_index,
    kernel_table,
    group_of,
    calib_gain,
):
    lines = lax.axis_size("line")
    chans = lax.axis_size("chan")
    me = lax.axis_index("line")
    _, cl, rows, na = current_image.shape
    p_len = 128 if na % 128 == 0 else 1
    q_len = na // p_len

    levels = jnp.arange(G, dtype=jnp.int32)
    channel_gain = jnp.sum(
        (group_of[:, None] == levels[None, :]).astype(jnp.float32) * calib_gain[None, :], axis=1
    )

    local_taps = tap_table(tap_index, kernel_table)
    local_weights = shift_weights(range_offset, local_taps)
    angles = doppler_phase[None, :, :] + channel_ramp[:, None, :]
    cos_a = jnp.cos(angles)
    sin_a = jnp.sin(angles)
    gain = channel_gain[:, None, None]
    back_r = gain * (cos_a * observed[0] + sin_a * observed[1])
    back_i = gain * (cos_a * observed[1] - sin_a * observed[0])
    data = adjoint_shift(jnp.stack([back_r, back_i]), local_weights)
    data = data * (step_length / math.sqrt(na))
    packed = lax.all_gather(jnp.stack([tap_index, range_offset]), "line", axis=1, tiled=True)
    packed, data = lax.optimization_barrier((packed, data))
    data = lax.all_to_all(data, "line", split_axis=2, concat_axis=3, tiled=True)
    data = data.reshape(2, cl, rows, q_len, p_len).swapaxes(-1, -2)

    taps = tap_table(packed[0], kernel_table)
    weights = shift_weights(packed[1], taps)

    def spectral(v):
        return v.reshape(v.shape[:-1] + (q_len, p_len)).swapaxes(-1, -2)

    weights = spectral(weights)
    band = [
        spectral(sum(taps[:, k] * taps[:, k + e] for k in range(K - e))) for e in range(K)
    ]
    coef = (channel_gain * channel_gain) * (step_length / na)

    momenta = momentum_weights()
    earlier = previous_image
    latest = current_image
    forward_pairs = [(i, i + 1) for i in range(lines - 1)]
    backward_pairs = [(i + 1, i) for i in range(lines - 1)]
    first = (me == 0)
    last = (me == lines - 1)

    def wgt(d):
        return weights[d - LOWEST]

    for iteration in range(ITERS):
        blended = latest + momenta[iteration] * (latest - earlier)
        low = lax.ppermute(blended[:, :, rows - HALO :], "line", forward_pairs)
        high = lax.ppermute(blended[:, :, :HALO], "line", backward_pairs)
        ext = jnp.concatenate([low, blended, high], axis=2)
        ext_rows = rows + 2 * HALO
        spec = forward_transform(ext.reshape(2, -1, p_len, q_len), p_len, q_len)
        spec = spec.reshape(2, cl, ext_rows, p_len, q_len)

        def at(r):
            return spec[:, :, r]

        gram = []
        for r in range(rows):
            c = r + HALO
            acc = band[0] * at(c)
            for e in range(1, K):
                acc = acc + band[e] * (at(c - e) + at(c + e))
            gram.append(acc)
        low_fix = []
        for rr in range(K):
            acc = None
            for s in range(1, K + 1):
                if rr + s > OFFMAX + K // 2:
                    continue
                u = None
                for j in range(K):
                    if j + s > OFFMAX + K // 2:
                        continue
                    term = wgt(j + s) * at(HALO + j)
                    u = term if u is None else u + term
                term = wgt(rr + s) * u
                acc = term if acc is None else acc + term
            low_fix.append(acc)
        high_fix = []
        for tt in range(-(K - 2), 1):
            acc = None
            for s in range(1, K):
                if tt - s < LOWEST:
                    continue
                u = None
                for t in range(-(K - 2), 1):
                    if t - s < LOWEST:
                        continue
                    term = wgt(t - s) * at(HALO + rows - 1 + t)
                    u = term if u is None else u + term
                term = wgt(tt - s) * u
                acc = term if acc is None else acc + term
            high_fix.append(acc)
        for rr in range(K):
            gram[rr] = gram[rr] - jnp.where(first, low_fix[rr], 0.0)
        for idx, tt in enumerate(range(-(K - 2), 1)):
            r = rows - 1 + tt
            gram[r] = gram[r] - jnp.where(last, high_fix[idx], 0.0)
        gram = jnp.stack(gram, axis=2)
        resid = coef[None, :, None, None, None] * gram - data
        grad = inverse_transform(resid.reshape(2, -1, p_len, q_len), p_len, q_len)
        shifted = blended - grad.reshape(blended.shape)
        squares = jnp.sum(shifted * shifted, axis=(0, 1))
        if chans == 2:
            squares = squares + lax.ppermute(squares, "chan", [(0, 1), (1, 0)])
        else:
            squares = lax.psum(squares, "chan")
        factor = shrink(squares)
        earlier = latest
        latest = shifted * factor[None, None]
    return (latest, earlier)


def solution(mesh):
    in_specs = (
        P(None, "chan", None, "line"),
        P(None, "chan", "line", None),
        P(None, "chan", "line", None),
        P(None, "line"),
        P("chan", "line"),
        P("line"),
        P("line"),
        P(),
        P("chan"),
        P(),
    )
    out_specs = (P(None, "chan", "line", None), P(None, "chan", "line", None))
    return jax.shard_map(body, mesh=mesh, in_specs=in_specs, out_specs=out_specs, check_vma=False)
```

```python
import math

import numpy as np
import jax
import jax.numpy as jnp
from jax import lax
from jax.sharding import PartitionSpec as P
from jax.experimental import pallas as pl

K = 4
Q = 16
OFFMAX = 2
G = 4
ITERS = 2
START_ITER = 8
HALO = K - 1

step_length = 0.25
threshold = 3.0


def momentum_weights():
    current = 1.0
    for counter in range(1, START_ITER):
        current = (1.0 + math.sqrt(1.0 + 4.0 * current * current)) / 2.0
    momenta = []
    for counter in range(ITERS):
        following = (1.0 + math.sqrt(1.0 + 4.0 * current * current)) / 2.0
        momenta.append((current - 1.0) / following)
        current = following
    return momenta


def tap_table(tap_index, kernel_table):
    levels = jnp.arange(Q, dtype=jnp.int32)
    onehot = (tap_index[:, None] == levels[None, :]).astype(jnp.float32)
    return jnp.dot(
        onehot, kernel_table, precision=lax.Precision.HIGHEST, preferred_element_type=jnp.float32
    )


def shift_weights(range_offset, tap_weights):
    stacked = []
    for displacement in range(-(OFFMAX + K // 2 - 1), OFFMAX + K // 2 + 1):
        summed = jnp.zeros(range_offset.shape, jnp.float32)
        for tap_number in range(K):
            matches = (range_offset + (tap_number - (K // 2 - 1)) == displacement).astype(
                jnp.float32
            )
            summed = summed + tap_weights[..., tap_number] * matches
        stacked.append(summed)
    return jnp.stack(stacked)


LOWEST = -(OFFMAX + K // 2 - 1)


def adjoint_shift(rows, weights):
    rim_width = OFFMAX + K // 2
    count = rows.shape[-2]
    pad = [(0, 0)] * rows.ndim
    pad[-2] = (rim_width, rim_width)
    padded = jnp.pad(rows, pad)
    summed = None
    for position in range(weights.shape[0]):
        displacement = LOWEST + position
        anchor = rim_width - displacement
        sliced = lax.slice_in_dim(padded, anchor, anchor + count, axis=rows.ndim - 2)
        weighted = sliced * weights[position]
        summed = weighted if summed is None else summed + weighted
    return summed


def left_block(count, sign):
    counter = np.arange(count)
    angle = (np.outer(counter, counter) % count) * (2.0 * np.pi / count)
    c = np.cos(angle)
    s = sign * np.sin(angle)
    return jnp.asarray(np.block([[c, -s], [s, c]]), jnp.float32)


def right_block(count, sign):
    counter = np.arange(count)
    angle = (np.outer(counter, counter) % count) * (2.0 * np.pi / count)
    c = np.cos(angle)
    s = sign * np.sin(angle)
    return jnp.asarray(np.block([[c, s], [-s, c]]), jnp.float32)


def twiddle(rows, cols, total, sign):
    angle = (np.outer(np.arange(rows), np.arange(cols)) % total) * (2.0 * np.pi / total)
    return jnp.asarray(np.stack([np.cos(angle), sign * np.sin(angle)]), jnp.float32)


def dot(a, b):
    return jnp.dot(a, b, precision=lax.Precision.HIGHEST, preferred_element_type=jnp.float32)


def forward_kernel(x_ref, w_ref, v_ref, t_ref, o_ref):
    nb, p_len, q_len = x_ref.shape[1], x_ref.shape[2], x_ref.shape[3]
    stacked = jnp.concatenate(
        [
            jnp.concatenate([x_ref[0, b] for b in range(nb)], axis=1),
            jnp.concatenate([x_ref[1, b] for b in range(nb)], axis=1),
        ],
        axis=0,
    )
    mid = dot(w_ref[...], stacked)
    tc = jnp.concatenate([t_ref[0]] * nb, axis=1)
    ts = jnp.concatenate([t_ref[1]] * nb, axis=1)
    mr = mid[:p_len]
    mi = mid[p_len:]
    tr = mr * tc - mi * ts
    ti = mi * tc + mr * ts
    turned = jnp.concatenate(
        [
            jnp.concatenate([tr[:, b * q_len : (b + 1) * q_len], ti[:, b * q_len : (b + 1) * q_len]], axis=1)
            for b in range(nb)
        ],
        axis=0,
    )
    out = dot(turned, v_ref[...])
    for b in range(nb):
        o_ref[0, b] = out[b * p_len : (b + 1) * p_len, :q_len]
        o_ref[1, b] = out[b * p_len : (b + 1) * p_len, q_len:]


def inverse_kernel(y_ref, v_ref, w_ref, t_ref, o_ref):
    nb, p_len, q_len = y_ref.shape[1], y_ref.shape[2], y_ref.shape[3]
    stacked = jnp.concatenate(
        [jnp.concatenate([y_ref[0, b], y_ref[1, b]], axis=1) for b in range(nb)], axis=0
    )
    mid = dot(stacked, v_ref[...])
    tc = jnp.concatenate([t_ref[0]] * nb, axis=0)
    ts = jnp.concatenate([t_ref[1]] * nb, axis=0)
    mr = mid[:, :q_len]
    mi = mid[:, q_len:]
    tr = mr * tc - mi * ts
    ti = mi * tc + mr * ts
    turned = jnp.concatenate(
        [
            jnp.concatenate([tr[b * p_len : (b + 1) * p_len] for b in range(nb)], axis=1),
            jnp.concatenate([ti[b * p_len : (b + 1) * p_len] for b in range(nb)], axis=1),
        ],
        axis=0,
    )
    out = dot(w_ref[...], turned)
    for b in range(nb):
        o_ref[0, b] = out[:p_len, b * q_len : (b + 1) * q_len]
        o_ref[1, b] = out[p_len:, b * q_len : (b + 1) * q_len]


def transpose_kernel(x_ref, o_ref):
    for b in range(x_ref.shape[0]):
        o_ref[b] = x_ref[b].T


def swap_minor(x):
    total, p_len, q_len = x.shape
    nb = block_count(total)
    return pl.pallas_call(
        transpose_kernel,
        out_shape=jax.ShapeDtypeStruct((total, q_len, p_len), x.dtype),
        grid=(total // nb,),
        in_specs=[pl.BlockSpec((nb, p_len, q_len), lambda i: (i, 0, 0))],
        out_specs=pl.BlockSpec((nb, q_len, p_len), lambda i: (i, 0, 0)),
        cost_estimate=pl.CostEstimate(flops=0, bytes_accessed=2 * x.size * 4, transcendentals=0),
    )(x)


def block_count(total):
    for nb in (8, 7, 6, 5, 4, 3, 2, 1):
        if total % nb == 0:
            return nb
    return 1


def run_transform(kernel, data, first, second, turn):
    _, total, p_len, q_len = data.shape
    nb = block_count(total)
    flops = 2 * 2 * total * (2 * p_len) * (2 * q_len) * (p_len + q_len) // 2
    return pl.pallas_call(
        kernel,
        out_shape=jax.ShapeDtypeStruct(data.shape, jnp.float32),
        grid=(total // nb,),
        in_specs=[
            pl.BlockSpec((2, nb, p_len, q_len), lambda i: (0, i, 0, 0)),
            pl.BlockSpec(first.shape, lambda i: (0, 0)),
            pl.BlockSpec(second.shape, lambda i: (0, 0)),
            pl.BlockSpec(turn.shape, lambda i: (0, 0, 0)),
        ],
        out_specs=pl.BlockSpec((2, nb, p_len, q_len), lambda i: (0, i, 0, 0)),
        cost_estimate=pl.CostEstimate(
            flops=flops, bytes_accessed=2 * data.size * 4, transcendentals=0
        ),
    )(data, first, second, turn)


def forward_transform(x, p_len, q_len):
    return run_transform(
        forward_kernel,
        x,
        left_block(p_len, -1.0),
        right_block(q_len, -1.0),
        twiddle(p_len, q_len, p_len * q_len, -1.0),
    )


def inverse_transform(y, p_len, q_len):
    return run_transform(
        inverse_kernel,
        y,
        right_block(q_len, 1.0),
        left_block(p_len, 1.0),
        twiddle(p_len, q_len, p_len * q_len, 1.0),
    )


def shrink(squares):
    magnitude = jnp.sqrt(squares)
    return jnp.maximum(magnitude - threshold, 0.0) / jnp.maximum(magnitude, threshold)


def body(
    observed,
    current_image,
    previous_image,
    doppler_phase,
    channel_ramp,
    range_offset,
    tap_index,
    kernel_table,
    group_of,
    calib_gain,
):
    lines = lax.axis_size("line")
    chans = lax.axis_size("chan")
    me = lax.axis_index("line")
    _, cl, rows, na = current_image.shape
    p_len = 128 if na % 128 == 0 else 1
    q_len = na // p_len

    levels = jnp.arange(G, dtype=jnp.int32)
    channel_gain = jnp.sum(
        (group_of[:, None] == levels[None, :]).astype(jnp.float32) * calib_gain[None, :], axis=1
    )

    local_taps = tap_table(tap_index, kernel_table)
    local_weights = shift_weights(range_offset, local_taps)
    angles = doppler_phase[None, :, :] + channel_ramp[:, None, :]
    cos_a = jnp.cos(angles)
    sin_a = jnp.sin(angles)
    gain = channel_gain[:, None, None]
    back_r = gain * (cos_a * observed[0] + sin_a * observed[1])
    back_i = gain * (cos_a * observed[1] - sin_a * observed[0])
    data = adjoint_shift(jnp.stack([back_r, back_i]), local_weights)
    data = data * (step_length / math.sqrt(na))
    extra = jnp.stack(
        [
            jnp.broadcast_to(tap_index.astype(jnp.float32)[None, :], data.shape[2:]),
            jnp.broadcast_to(range_offset.astype(jnp.float32)[None, :], data.shape[2:]),
        ]
    )[:, None]
    payload = jnp.concatenate([data, extra], axis=1)
    payload = lax.all_to_all(payload, "line", split_axis=2, concat_axis=3, tiled=True)
    data = swap_minor(payload[:, :cl].reshape(-1, q_len, p_len)).reshape(2, cl, rows, p_len, q_len)
    all_taps = payload[0, cl, 0].astype(jnp.int32)
    all_offsets = payload[1, cl, 0].astype(jnp.int32)
    taps = tap_table(all_taps, kernel_table)
    weights = shift_weights(all_offsets, taps)

    def spectral(v):
        return v.reshape(v.shape[:-1] + (q_len, p_len)).swapaxes(-1, -2)

    weights = spectral(weights)
    band = [
        spectral(sum(taps[:, k] * taps[:, k + e] for k in range(K - e))) for e in range(K)
    ]
    coef = (channel_gain * channel_gain) * (step_length / na)

    momenta = momentum_weights()
    earlier = previous_image.reshape(2, cl, rows, p_len, q_len)
    latest = current_image.reshape(2, cl, rows, p_len, q_len)
    forward_pairs = [(i, i + 1) for i in range(lines - 1)]
    backward_pairs = [(i + 1, i) for i in range(lines - 1)]
    first = (me == 0)
    last = (me == lines - 1)

    def wgt(d):
        return weights[d - LOWEST]

    for iteration in range(ITERS):
        blended = latest + momenta[iteration] * (latest - earlier)
        low = lax.ppermute(blended[:, :, rows - HALO :], "line", forward_pairs)
        high = lax.ppermute(blended[:, :, :HALO], "line", backward_pairs)
        own = forward_transform(blended.reshape(2, -1, p_len, q_len), p_len, q_len)
        own = own.reshape(2, cl, rows, p_len, q_len)
        rim = jnp.concatenate([low, high], axis=2)
        rim = forward_transform(rim.reshape(2, -1, p_len, q_len), p_len, q_len)
        rim = rim.reshape(2, cl, 2 * HALO, p_len, q_len)

        def at(r):
            if r < HALO:
                return rim[:, :, r]
            if r < HALO + rows:
                return own[:, :, r - HALO]
            return rim[:, :, r - rows]

        gram = []
        for r in range(rows):
            c = r + HALO
            acc = band[0] * at(c)
            for e in range(1, K):
                acc = acc + band[e] * (at(c - e) + at(c + e))
            gram.append(acc)
        low_fix = []
        for rr in range(K):
            acc = None
            for s in range(1, K + 1):
                if rr + s > OFFMAX + K // 2:
                    continue
                u = None
                for j in range(K):
                    if j + s > OFFMAX + K // 2:
                        continue
                    term = wgt(j + s) * at(HALO + j)
                    u = term if u is None else u + term
                term = wgt(rr + s) * u
                acc = term if acc is None else acc + term
            low_fix.append(acc)
        high_fix = []
        for tt in range(-(K - 2), 1):
            acc = None
            for s in range(1, K):
                if tt - s < LOWEST:
                    continue
                u = None
                for t in range(-(K - 2), 1):
                    if t - s < LOWEST:
                        continue
                    term = wgt(t - s) * at(HALO + rows - 1 + t)
                    u = term if u is None else u + term
                term = wgt(tt - s) * u
                acc = term if acc is None else acc + term
            high_fix.append(acc)
        for rr in range(K):
            gram[rr] = gram[rr] - jnp.where(first, low_fix[rr], 0.0)
        for idx, tt in enumerate(range(-(K - 2), 1)):
            r = rows - 1 + tt
            gram[r] = gram[r] - jnp.where(last, high_fix[idx], 0.0)
        gram = jnp.stack(gram, axis=2)
        resid = coef[None, :, None, None, None] * gram - data
        grad = inverse_transform(resid.reshape(2, -1, p_len, q_len), p_len, q_len)
        shifted = blended - grad.reshape(blended.shape)
        squares = jnp.sum(shifted * shifted, axis=(0, 1))
        if chans == 2:
            squares = squares + lax.ppermute(squares, "chan", [(0, 1), (1, 0)])
        else:
            squares = lax.psum(squares, "chan")
        factor = shrink(squares)
        earlier = latest
        latest = shifted * factor[None, None]
    return (latest.reshape(current_image.shape), earlier.reshape(current_image.shape))


def solution(mesh):
    in_specs = (
        P(None, "chan", None, "line"),
        P(None, "chan", "line", None),
        P(None, "chan", "line", None),
        P(None, "line"),
        P("chan", "line"),
        P("line"),
        P("line"),
        P(),
        P("chan"),
        P(),
    )
    out_specs = (P(None, "chan", "line", None), P(None, "chan", "line", None))
    return jax.shard_map(body, mesh=mesh, in_specs=in_specs, out_specs=out_specs, check_vma=False)
```

```python
import math

import numpy as np
import jax
import jax.numpy as jnp
from jax import lax
from jax.sharding import PartitionSpec as P
from jax.experimental import pallas as pl

K = 4
Q = 16
OFFMAX = 2
G = 4
ITERS = 2
START_ITER = 8
HALO = K - 1

step_length = 0.25
threshold = 3.0


def momentum_weights():
    current = 1.0
    for counter in range(1, START_ITER):
        current = (1.0 + math.sqrt(1.0 + 4.0 * current * current)) / 2.0
    momenta = []
    for counter in range(ITERS):
        following = (1.0 + math.sqrt(1.0 + 4.0 * current * current)) / 2.0
        momenta.append((current - 1.0) / following)
        current = following
    return momenta


def tap_table(tap_index, kernel_table):
    levels = jnp.arange(Q, dtype=jnp.int32)
    onehot = (tap_index[:, None] == levels[None, :]).astype(jnp.float32)
    return jnp.dot(
        onehot, kernel_table, precision=lax.Precision.HIGHEST, preferred_element_type=jnp.float32
    )


def shift_weights(range_offset, tap_weights):
    stacked = []
    for displacement in range(-(OFFMAX + K // 2 - 1), OFFMAX + K // 2 + 1):
        summed = jnp.zeros(range_offset.shape, jnp.float32)
        for tap_number in range(K):
            matches = (range_offset + (tap_number - (K // 2 - 1)) == displacement).astype(
                jnp.float32
            )
            summed = summed + tap_weights[..., tap_number] * matches
        stacked.append(summed)
    return jnp.stack(stacked)


LOWEST = -(OFFMAX + K // 2 - 1)


def adjoint_shift(rows, weights):
    rim_width = OFFMAX + K // 2
    count = rows.shape[-2]
    pad = [(0, 0)] * rows.ndim
    pad[-2] = (rim_width, rim_width)
    padded = jnp.pad(rows, pad)
    summed = None
    for position in range(weights.shape[0]):
        displacement = LOWEST + position
        anchor = rim_width - displacement
        sliced = lax.slice_in_dim(padded, anchor, anchor + count, axis=rows.ndim - 2)
        weighted = sliced * weights[position]
        summed = weighted if summed is None else summed + weighted
    return summed


def left_block(count, sign):
    counter = np.arange(count)
    angle = (np.outer(counter, counter) % count) * (2.0 * np.pi / count)
    c = np.cos(angle)
    s = sign * np.sin(angle)
    return jnp.asarray(np.block([[c, -s], [s, c]]), jnp.float32)


def right_block(count, sign):
    counter = np.arange(count)
    angle = (np.outer(counter, counter) % count) * (2.0 * np.pi / count)
    c = np.cos(angle)
    s = sign * np.sin(angle)
    return jnp.asarray(np.block([[c, s], [-s, c]]), jnp.float32)


def twiddle(rows, cols, total, sign):
    angle = (np.outer(np.arange(rows), np.arange(cols)) % total) * (2.0 * np.pi / total)
    return jnp.asarray(np.stack([np.cos(angle), sign * np.sin(angle)]), jnp.float32)


def dot(a, b):
    return jnp.dot(a, b, precision=lax.Precision.HIGHEST, preferred_element_type=jnp.float32)


def forward_kernel(x_ref, w_ref, v_ref, t_ref, o_ref):
    nb, p_len, q_len = x_ref.shape[1], x_ref.shape[2], x_ref.shape[3]
    stacked = jnp.concatenate(
        [
            jnp.concatenate([x_ref[0, b] for b in range(nb)], axis=1),
            jnp.concatenate([x_ref[1, b] for b in range(nb)], axis=1),
        ],
        axis=0,
    )
    mid = dot(w_ref[...], stacked)
    tc = jnp.concatenate([t_ref[0]] * nb, axis=1)
    ts = jnp.concatenate([t_ref[1]] * nb, axis=1)
    mr = mid[:p_len]
    mi = mid[p_len:]
    tr = mr * tc - mi * ts
    ti = mi * tc + mr * ts
    turned = jnp.concatenate(
        [
            jnp.concatenate([tr[:, b * q_len : (b + 1) * q_len], ti[:, b * q_len : (b + 1) * q_len]], axis=1)
            for b in range(nb)
        ],
        axis=0,
    )
    out = dot(turned, v_ref[...])
    for b in range(nb):
        o_ref[0, b] = out[b * p_len : (b + 1) * p_len, :q_len]
        o_ref[1, b] = out[b * p_len : (b + 1) * p_len, q_len:]


def inverse_kernel(y_ref, v_ref, w_ref, t_ref, o_ref):
    nb, p_len, q_len = y_ref.shape[1], y_ref.shape[2], y_ref.shape[3]
    stacked = jnp.concatenate(
        [jnp.concatenate([y_ref[0, b], y_ref[1, b]], axis=1) for b in range(nb)], axis=0
    )
    mid = dot(stacked, v_ref[...])
    tc = jnp.concatenate([t_ref[0]] * nb, axis=0)
    ts = jnp.concatenate([t_ref[1]] * nb, axis=0)
    mr = mid[:, :q_len]
    mi = mid[:, q_len:]
    tr = mr * tc - mi * ts
    ti = mi * tc + mr * ts
    turned = jnp.concatenate(
        [
            jnp.concatenate([tr[b * p_len : (b + 1) * p_len] for b in range(nb)], axis=1),
            jnp.concatenate([ti[b * p_len : (b + 1) * p_len] for b in range(nb)], axis=1),
        ],
        axis=0,
    )
    out = dot(w_ref[...], turned)
    for b in range(nb):
        o_ref[0, b] = out[:p_len, b * q_len : (b + 1) * q_len]
        o_ref[1, b] = out[p_len:, b * q_len : (b + 1) * q_len]


def transpose_kernel(x_ref, o_ref):
    for b in range(x_ref.shape[0]):
        o_ref[b] = x_ref[b].T


def swap_minor(x):
    total, p_len, q_len = x.shape
    nb = block_count(total)
    return pl.pallas_call(
        transpose_kernel,
        out_shape=jax.ShapeDtypeStruct((total, q_len, p_len), x.dtype),
        grid=(total // nb,),
        in_specs=[pl.BlockSpec((nb, p_len, q_len), lambda i: (i, 0, 0))],
        out_specs=pl.BlockSpec((nb, q_len, p_len), lambda i: (i, 0, 0)),
        cost_estimate=pl.CostEstimate(flops=0, bytes_accessed=2 * x.size * 4, transcendentals=0),
    )(x)


def block_count(total):
    for nb in (8, 7, 6, 5, 4, 3, 2, 1):
        if total % nb == 0:
            return nb
    return 1


def run_transform(kernel, data, first, second, turn):
    _, total, p_len, q_len = data.shape
    nb = block_count(total)
    flops = 2 * 2 * total * (2 * p_len) * (2 * q_len) * (p_len + q_len) // 2
    return pl.pallas_call(
        kernel,
        out_shape=jax.ShapeDtypeStruct(data.shape, jnp.float32),
        grid=(total // nb,),
        in_specs=[
            pl.BlockSpec((2, nb, p_len, q_len), lambda i: (0, i, 0, 0)),
            pl.BlockSpec(first.shape, lambda i: (0, 0)),
            pl.BlockSpec(second.shape, lambda i: (0, 0)),
            pl.BlockSpec(turn.shape, lambda i: (0, 0, 0)),
        ],
        out_specs=pl.BlockSpec((2, nb, p_len, q_len), lambda i: (0, i, 0, 0)),
        cost_estimate=pl.CostEstimate(
            flops=flops, bytes_accessed=2 * data.size * 4, transcendentals=0
        ),
    )(data, first, second, turn)


def forward_transform(x, p_len, q_len):
    return run_transform(
        forward_kernel,
        x,
        left_block(p_len, -1.0),
        right_block(q_len, -1.0),
        twiddle(p_len, q_len, p_len * q_len, -1.0),
    )


def inverse_transform(y, p_len, q_len):
    return run_transform(
        inverse_kernel,
        y,
        right_block(q_len, 1.0),
        left_block(p_len, 1.0),
        twiddle(p_len, q_len, p_len * q_len, 1.0),
    )


def shrink(squares):
    magnitude = jnp.sqrt(squares)
    return jnp.maximum(magnitude - threshold, 0.0) / jnp.maximum(magnitude, threshold)


def body(
    observed,
    current_image,
    previous_image,
    doppler_phase,
    channel_ramp,
    range_offset,
    tap_index,
    kernel_table,
    group_of,
    calib_gain,
):
    lines = lax.axis_size("line")
    chans = lax.axis_size("chan")
    me = lax.axis_index("line")
    _, cl, rows, na = current_image.shape
    p_len = 128 if na % 128 == 0 else 1
    q_len = na // p_len

    levels = jnp.arange(G, dtype=jnp.int32)
    channel_gain = jnp.sum(
        (group_of[:, None] == levels[None, :]).astype(jnp.float32) * calib_gain[None, :], axis=1
    )

    momenta = momentum_weights()
    earlier = previous_image.reshape(2, cl, rows, p_len, q_len)
    latest = current_image.reshape(2, cl, rows, p_len, q_len)
    forward_pairs = [(i, i + 1) for i in range(lines - 1)]
    backward_pairs = [(i + 1, i) for i in range(lines - 1)]

    packed = lax.all_gather(jnp.stack([tap_index, range_offset]), "line", axis=1, tiled=True)
    packed, latest, earlier = lax.optimization_barrier((packed, latest, earlier))
    taps = tap_table(packed[0], kernel_table)
    weights = shift_weights(packed[1], taps)

    blended = latest + momenta[0] * (latest - earlier)
    low = lax.ppermute(blended[:, :, rows - HALO :], "line", forward_pairs)
    high = lax.ppermute(blended[:, :, :HALO], "line", backward_pairs)

    local_taps = tap_table(tap_index, kernel_table)
    local_weights = shift_weights(range_offset, local_taps)
    angles = doppler_phase[None, :, :] + channel_ramp[:, None, :]
    cos_a = jnp.cos(angles)
    sin_a = jnp.sin(angles)
    gain = channel_gain[:, None, None]
    back_r = gain * (cos_a * observed[0] + sin_a * observed[1])
    back_i = gain * (cos_a * observed[1] - sin_a * observed[0])
    data = adjoint_shift(jnp.stack([back_r, back_i]), local_weights)
    data = data * (step_length / math.sqrt(na))
    data, low, high = lax.optimization_barrier((data, low, high))
    data = lax.all_to_all(data, "line", split_axis=2, concat_axis=3, tiled=True)

    def spectral(v):
        return v.reshape(v.shape[:-1] + (q_len, p_len)).swapaxes(-1, -2)

    weights = spectral(weights)
    band = [
        spectral(sum(taps[:, k] * taps[:, k + e] for k in range(K - e))) for e in range(K)
    ]
    coef = (channel_gain * channel_gain) * (step_length / na)

    first = (me == 0)
    last = (me == lines - 1)

    def wgt(d):
        return weights[d - LOWEST]

    undo = None
    for iteration in range(ITERS):
        if iteration > 0:
            blended = latest + momenta[iteration] * (latest - earlier)
            low = lax.ppermute(blended[:, :, rows - HALO :], "line", forward_pairs)
            high = lax.ppermute(blended[:, :, :HALO], "line", backward_pairs)
        own = forward_transform(blended.reshape(2, -1, p_len, q_len), p_len, q_len)
        own = own.reshape(2, cl, rows, p_len, q_len)
        rim = jnp.concatenate([low, high], axis=2)
        rim = forward_transform(rim.reshape(2, -1, p_len, q_len), p_len, q_len)
        rim = rim.reshape(2, cl, 2 * HALO, p_len, q_len)

        def at(r):
            if r < HALO:
                return rim[:, :, r]
            if r < HALO + rows:
                return own[:, :, r - HALO]
            return rim[:, :, r - rows]

        gram = []
        for r in range(rows):
            c = r + HALO
            acc = band[0] * at(c)
            for e in range(1, K):
                acc = acc + band[e] * (at(c - e) + at(c + e))
            gram.append(acc)
        low_fix = []
        for rr in range(K):
            acc = None
            for s in range(1, K + 1):
                if rr + s > OFFMAX + K // 2:
                    continue
                u = None
                for j in range(K):
                    if j + s > OFFMAX + K // 2:
                        continue
                    term = wgt(j + s) * at(HALO + j)
                    u = term if u is None else u + term
                term = wgt(rr + s) * u
                acc = term if acc is None else acc + term
            low_fix.append(acc)
        high_fix = []
        for tt in range(-(K - 2), 1):
            acc = None
            for s in range(1, K):
                if tt - s < LOWEST:
                    continue
                u = None
                for t in range(-(K - 2), 1):
                    if t - s < LOWEST:
                        continue
                    term = wgt(t - s) * at(HALO + rows - 1 + t)
                    u = term if u is None else u + term
                term = wgt(tt - s) * u
                acc = term if acc is None else acc + term
            high_fix.append(acc)
        for rr in range(K):
            gram[rr] = gram[rr] - jnp.where(first, low_fix[rr], 0.0)
        for idx, tt in enumerate(range(-(K - 2), 1)):
            r = rows - 1 + tt
            gram[r] = gram[r] - jnp.where(last, high_fix[idx], 0.0)
        gram = jnp.stack(gram, axis=2)
        resid = coef[None, :, None, None, None] * gram
        grad = inverse_transform(resid.reshape(2, -1, p_len, q_len), p_len, q_len)
        if undo is None:
            undo = swap_minor(data.reshape(-1, q_len, p_len))
            undo = inverse_transform(undo.reshape(2, -1, p_len, q_len), p_len, q_len)
            undo = undo.reshape(blended.shape)
        shifted = blended - grad.reshape(blended.shape) + undo
        squares = jnp.sum(shifted * shifted, axis=(0, 1))
        if chans == 2:
            squares = squares + lax.ppermute(squares, "chan", [(0, 1), (1, 0)])
        else:
            squares = lax.psum(squares, "chan")
        factor = shrink(squares)
        earlier = latest
        latest = shifted * factor[None, None]
    return (latest.reshape(current_image.shape), earlier.reshape(current_image.shape))


def solution(mesh):
    in_specs = (
        P(None, "chan", None, "line"),
        P(None, "chan", "line", None),
        P(None, "chan", "line", None),
        P(None, "line"),
        P("chan", "line"),
        P("line"),
        P("line"),
        P(),
        P("chan"),
        P(),
    )
    out_specs = (P(None, "chan", "line", None), P(None, "chan", "line", None))
    return jax.shard_map(body, mesh=mesh, in_specs=in_specs, out_specs=out_specs, check_vma=False)
```

```python
import math

import numpy as np
import jax
import jax.numpy as jnp
from jax import lax
from jax.sharding import PartitionSpec as P
from jax.experimental import pallas as pl

K = 4
Q = 16
OFFMAX = 2
G = 4
ITERS = 2
START_ITER = 8
HALO = K - 1

step_length = 0.25
threshold = 3.0


def momentum_weights():
    current = 1.0
    for counter in range(1, START_ITER):
        current = (1.0 + math.sqrt(1.0 + 4.0 * current * current)) / 2.0
    momenta = []
    for counter in range(ITERS):
        following = (1.0 + math.sqrt(1.0 + 4.0 * current * current)) / 2.0
        momenta.append((current - 1.0) / following)
        current = following
    return momenta


def tap_table(tap_index, kernel_table):
    levels = jnp.arange(Q, dtype=jnp.int32)
    onehot = (tap_index[:, None] == levels[None, :]).astype(jnp.float32)
    return jnp.dot(
        onehot, kernel_table, precision=lax.Precision.HIGHEST, preferred_element_type=jnp.float32
    )


def shift_weights(range_offset, tap_weights):
    stacked = []
    for displacement in range(-(OFFMAX + K // 2 - 1), OFFMAX + K // 2 + 1):
        summed = jnp.zeros(range_offset.shape, jnp.float32)
        for tap_number in range(K):
            matches = (range_offset + (tap_number - (K // 2 - 1)) == displacement).astype(
                jnp.float32
            )
            summed = summed + tap_weights[..., tap_number] * matches
        stacked.append(summed)
    return jnp.stack(stacked)


LOWEST = -(OFFMAX + K // 2 - 1)


def adjoint_shift(rows, weights):
    rim_width = OFFMAX + K // 2
    count = rows.shape[-2]
    pad = [(0, 0)] * rows.ndim
    pad[-2] = (rim_width, rim_width)
    padded = jnp.pad(rows, pad)
    summed = None
    for position in range(weights.shape[0]):
        displacement = LOWEST + position
        anchor = rim_width - displacement
        sliced = lax.slice_in_dim(padded, anchor, anchor + count, axis=rows.ndim - 2)
        weighted = sliced * weights[position]
        summed = weighted if summed is None else summed + weighted
    return summed


def left_block(count, sign):
    counter = np.arange(count)
    angle = (np.outer(counter, counter) % count) * (2.0 * np.pi / count)
    c = np.cos(angle)
    s = sign * np.sin(angle)
    return jnp.asarray(np.block([[c, -s], [s, c]]), jnp.float32)


def right_block(count, sign):
    counter = np.arange(count)
    angle = (np.outer(counter, counter) % count) * (2.0 * np.pi / count)
    c = np.cos(angle)
    s = sign * np.sin(angle)
    return jnp.asarray(np.block([[c, s], [-s, c]]), jnp.float32)


def twiddle(rows, cols, total, sign):
    angle = (np.outer(np.arange(rows), np.arange(cols)) % total) * (2.0 * np.pi / total)
    return jnp.asarray(np.stack([np.cos(angle), sign * np.sin(angle)]), jnp.float32)


def dot(a, b):
    return jnp.dot(a, b, precision=lax.Precision.HIGHEST, preferred_element_type=jnp.float32)


def forward_kernel(x_ref, w_ref, v_ref, t_ref, o_ref):
    nb, p_len, q_len = x_ref.shape[1], x_ref.shape[2], x_ref.shape[3]
    stacked = jnp.concatenate(
        [
            jnp.concatenate([x_ref[0, b] for b in range(nb)], axis=1),
            jnp.concatenate([x_ref[1, b] for b in range(nb)], axis=1),
        ],
        axis=0,
    )
    mid = dot(w_ref[...], stacked)
    tc = jnp.concatenate([t_ref[0]] * nb, axis=1)
    ts = jnp.concatenate([t_ref[1]] * nb, axis=1)
    mr = mid[:p_len]
    mi = mid[p_len:]
    tr = mr * tc - mi * ts
    ti = mi * tc + mr * ts
    turned = jnp.concatenate(
        [
            jnp.concatenate([tr[:, b * q_len : (b + 1) * q_len], ti[:, b * q_len : (b + 1) * q_len]], axis=1)
            for b in range(nb)
        ],
        axis=0,
    )
    out = dot(turned, v_ref[...])
    for b in range(nb):
        o_ref[0, b] = out[b * p_len : (b + 1) * p_len, :q_len]
        o_ref[1, b] = out[b * p_len : (b + 1) * p_len, q_len:]


def inverse_kernel(y_ref, v_ref, w_ref, t_ref, o_ref):
    nb, p_len, q_len = y_ref.shape[1], y_ref.shape[2], y_ref.shape[3]
    stacked = jnp.concatenate(
        [jnp.concatenate([y_ref[0, b], y_ref[1, b]], axis=1) for b in range(nb)], axis=0
    )
    mid = dot(stacked, v_ref[...])
    tc = jnp.concatenate([t_ref[0]] * nb, axis=0)
    ts = jnp.concatenate([t_ref[1]] * nb, axis=0)
    mr = mid[:, :q_len]
    mi = mid[:, q_len:]
    tr = mr * tc - mi * ts
    ti = mi * tc + mr * ts
    turned = jnp.concatenate(
        [
            jnp.concatenate([tr[b * p_len : (b + 1) * p_len] for b in range(nb)], axis=1),
            jnp.concatenate([ti[b * p_len : (b + 1) * p_len] for b in range(nb)], axis=1),
        ],
        axis=0,
    )
    out = dot(w_ref[...], turned)
    for b in range(nb):
        o_ref[0, b] = out[:p_len, b * q_len : (b + 1) * q_len]
        o_ref[1, b] = out[p_len:, b * q_len : (b + 1) * q_len]


def transpose_kernel(x_ref, o_ref):
    for b in range(x_ref.shape[0]):
        o_ref[b] = x_ref[b].T


def swap_minor(x):
    total, p_len, q_len = x.shape
    nb = block_count(total)
    return pl.pallas_call(
        transpose_kernel,
        out_shape=jax.ShapeDtypeStruct((total, q_len, p_len), x.dtype),
        grid=(total // nb,),
        in_specs=[pl.BlockSpec((nb, p_len, q_len), lambda i: (i, 0, 0))],
        out_specs=pl.BlockSpec((nb, q_len, p_len), lambda i: (i, 0, 0)),
        cost_estimate=pl.CostEstimate(flops=0, bytes_accessed=2 * x.size * 4, transcendentals=0),
    )(x)


def block_count(total):
    for nb in (8, 7, 6, 5, 4, 3, 2, 1):
        if total % nb == 0:
            return nb
    return 1


def run_transform(kernel, data, first, second, turn):
    _, total, p_len, q_len = data.shape
    nb = block_count(total)
    flops = 2 * 2 * total * (2 * p_len) * (2 * q_len) * (p_len + q_len) // 2
    return pl.pallas_call(
        kernel,
        out_shape=jax.ShapeDtypeStruct(data.shape, jnp.float32),
        grid=(total // nb,),
        in_specs=[
            pl.BlockSpec((2, nb, p_len, q_len), lambda i: (0, i, 0, 0)),
            pl.BlockSpec(first.shape, lambda i: (0, 0)),
            pl.BlockSpec(second.shape, lambda i: (0, 0)),
            pl.BlockSpec(turn.shape, lambda i: (0, 0, 0)),
        ],
        out_specs=pl.BlockSpec((2, nb, p_len, q_len), lambda i: (0, i, 0, 0)),
        cost_estimate=pl.CostEstimate(
            flops=flops, bytes_accessed=2 * data.size * 4, transcendentals=0
        ),
    )(data, first, second, turn)


def forward_transform(x, p_len, q_len):
    return run_transform(
        forward_kernel,
        x,
        left_block(p_len, -1.0),
        right_block(q_len, -1.0),
        twiddle(p_len, q_len, p_len * q_len, -1.0),
    )


def inverse_transform(y, p_len, q_len):
    return run_transform(
        inverse_kernel,
        y,
        right_block(q_len, 1.0),
        left_block(p_len, 1.0),
        twiddle(p_len, q_len, p_len * q_len, 1.0),
    )


def shrink(squares):
    magnitude = jnp.sqrt(squares)
    return jnp.maximum(magnitude - threshold, 0.0) / jnp.maximum(magnitude, threshold)


def body(
    observed,
    current_image,
    previous_image,
    doppler_phase,
    channel_ramp,
    range_offset,
    tap_index,
    kernel_table,
    group_of,
    calib_gain,
):
    lines = lax.axis_size("line")
    chans = lax.axis_size("chan")
    me = lax.axis_index("line")
    _, cl, rows, na = current_image.shape
    p_len = 128 if na % 128 == 0 else 1
    q_len = na // p_len

    levels = jnp.arange(G, dtype=jnp.int32)
    channel_gain = jnp.sum(
        (group_of[:, None] == levels[None, :]).astype(jnp.float32) * calib_gain[None, :], axis=1
    )

    momenta = momentum_weights()
    forward_pairs = [(i, i + 1) for i in range(lines - 1)]
    backward_pairs = [(i + 1, i) for i in range(lines - 1)]

    def edge_blend(lo, hi):
        cur = current_image[:, :, lo:hi]
        return cur + momenta[0] * (cur - previous_image[:, :, lo:hi])

    low = lax.ppermute(edge_blend(rows - HALO, rows), "line", forward_pairs)
    high = lax.ppermute(edge_blend(0, HALO), "line", backward_pairs)

    table = jnp.stack([tap_index, range_offset])
    table = jnp.broadcast_to(table[None], (lines,) + table.shape)
    table = lax.all_to_all(table, "line", split_axis=0, concat_axis=2, tiled=True)[0]

    earlier = previous_image.reshape(2, cl, rows, p_len, q_len)
    latest = current_image.reshape(2, cl, rows, p_len, q_len)
    blended = latest + momenta[0] * (latest - earlier)

    local_taps = tap_table(tap_index, kernel_table)
    local_weights = shift_weights(range_offset, local_taps)
    angles = doppler_phase[None, :, :] + channel_ramp[:, None, :]
    cos_a = jnp.cos(angles)
    sin_a = jnp.sin(angles)
    gain = channel_gain[:, None, None]
    back_r = gain * (cos_a * observed[0] + sin_a * observed[1])
    back_i = gain * (cos_a * observed[1] - sin_a * observed[0])
    data = adjoint_shift(jnp.stack([back_r, back_i]), local_weights)
    data = data * (step_length / math.sqrt(na))
    data, low, high, table = lax.optimization_barrier((data, low, high, table))
    data = data.reshape(2, cl, data.shape[2], data.shape[3] // p_len, p_len)
    data = lax.all_to_all(data, "line", split_axis=2, concat_axis=3, tiled=True)
    taps = tap_table(table[0], kernel_table)
    weights = shift_weights(table[1], taps)

    def spectral(v):
        return v.reshape(v.shape[:-1] + (q_len, p_len)).swapaxes(-1, -2)

    weights = spectral(weights)
    band = [
        spectral(sum(taps[:, k] * taps[:, k + e] for k in range(K - e))) for e in range(K)
    ]
    coef = (channel_gain * channel_gain) * (step_length / na)

    first = (me == 0)
    last = (me == lines - 1)

    def wgt(d):
        return weights[d - LOWEST]

    undo = None
    for iteration in range(ITERS):
        if iteration > 0:
            blended = latest + momenta[iteration] * (latest - earlier)
            low = lax.ppermute(blended[:, :, rows - HALO :], "line", forward_pairs)
            high = lax.ppermute(blended[:, :, :HALO], "line", backward_pairs)
            if iteration == ITERS - 1:
                prior = latest.reshape(current_image.shape)
                low, high, prior = lax.optimization_barrier((low, high, prior))
        elif ITERS == 1:
            prior = current_image
        own = forward_transform(blended.reshape(2, -1, p_len, q_len), p_len, q_len)
        own = own.reshape(2, cl, rows, p_len, q_len)
        rim = jnp.concatenate([low, high], axis=2).reshape(2, -1, p_len, q_len)
        rim = forward_transform(rim, p_len, q_len)
        rim = rim.reshape(2, cl, 2 * HALO, p_len, q_len)

        def at(r):
            if r < HALO:
                return rim[:, :, r]
            if r < HALO + rows:
                return own[:, :, r - HALO]
            return rim[:, :, r - rows]

        gram = []
        for r in range(rows):
            c = r + HALO
            acc = band[0] * at(c)
            for e in range(1, K):
                acc = acc + band[e] * (at(c - e) + at(c + e))
            gram.append(acc)
        low_fix = []
        for rr in range(K):
            acc = None
            for s in range(1, K + 1):
                if rr + s > OFFMAX + K // 2:
                    continue
                u = None
                for j in range(K):
                    if j + s > OFFMAX + K // 2:
                        continue
                    term = wgt(j + s) * at(HALO + j)
                    u = term if u is None else u + term
                term = wgt(rr + s) * u
                acc = term if acc is None else acc + term
            low_fix.append(acc)
        high_fix = []
        for tt in range(-(K - 2), 1):
            acc = None
            for s in range(1, K):
                if tt - s < LOWEST:
                    continue
                u = None
                for t in range(-(K - 2), 1):
                    if t - s < LOWEST:
                        continue
                    term = wgt(t - s) * at(HALO + rows - 1 + t)
                    u = term if u is None else u + term
                term = wgt(tt - s) * u
                acc = term if acc is None else acc + term
            high_fix.append(acc)
        for rr in range(K):
            gram[rr] = gram[rr] - jnp.where(first, low_fix[rr], 0.0)
        for idx, tt in enumerate(range(-(K - 2), 1)):
            r = rows - 1 + tt
            gram[r] = gram[r] - jnp.where(last, high_fix[idx], 0.0)
        gram = jnp.stack(gram, axis=2)
        resid = coef[None, :, None, None, None] * gram
        grad = inverse_transform(resid.reshape(2, -1, p_len, q_len), p_len, q_len)
        if undo is None:
            undo = swap_minor(data.reshape(-1, q_len, p_len))
            undo = inverse_transform(undo.reshape(2, -1, p_len, q_len), p_len, q_len)
            undo = undo.reshape(blended.shape)
        shifted = blended - grad.reshape(blended.shape) + undo
        squares = jnp.sum(shifted * shifted, axis=(0, 1))
        if chans == 2:
            squares = squares + lax.ppermute(squares, "chan", [(0, 1), (1, 0)])
        else:
            squares = lax.psum(squares, "chan")
        factor = shrink(squares)
        earlier = latest
        latest = shifted * factor[None, None]
    return (latest.reshape(current_image.shape), prior)


def solution(mesh):
    in_specs = (
        P(None, "chan", None, "line"),
        P(None, "chan", "line", None),
        P(None, "chan", "line", None),
        P(None, "line"),
        P("chan", "line"),
        P("line"),
        P("line"),
        P(),
        P("chan"),
        P(),
    )
    out_specs = (P(None, "chan", "line", None), P(None, "chan", "line", None))
    return jax.shard_map(body, mesh=mesh, in_specs=in_specs, out_specs=out_specs, check_vma=False)
```

```python
import math

import numpy as np
import jax
import jax.numpy as jnp
from jax import lax
from jax.sharding import PartitionSpec as P
from jax.experimental import pallas as pl

K = 4
Q = 16
OFFMAX = 2
G = 4
ITERS = 2
START_ITER = 8
HALO = K - 1

step_length = 0.25
threshold = 3.0


def momentum_weights():
    current = 1.0
    for counter in range(1, START_ITER):
        current = (1.0 + math.sqrt(1.0 + 4.0 * current * current)) / 2.0
    momenta = []
    for counter in range(ITERS):
        following = (1.0 + math.sqrt(1.0 + 4.0 * current * current)) / 2.0
        momenta.append((current - 1.0) / following)
        current = following
    return momenta


def tap_table(tap_index, kernel_table):
    levels = jnp.arange(Q, dtype=jnp.int32)
    onehot = (tap_index[:, None] == levels[None, :]).astype(jnp.float32)
    return jnp.dot(
        onehot, kernel_table, precision=lax.Precision.HIGHEST, preferred_element_type=jnp.float32
    )


def shift_weights(range_offset, tap_weights):
    stacked = []
    for displacement in range(-(OFFMAX + K // 2 - 1), OFFMAX + K // 2 + 1):
        summed = jnp.zeros(range_offset.shape, jnp.float32)
        for tap_number in range(K):
            matches = (range_offset + (tap_number - (K // 2 - 1)) == displacement).astype(
                jnp.float32
            )
            summed = summed + tap_weights[..., tap_number] * matches
        stacked.append(summed)
    return jnp.stack(stacked)


LOWEST = -(OFFMAX + K // 2 - 1)


def adjoint_shift(rows, weights):
    rim_width = OFFMAX + K // 2
    count = rows.shape[-2]
    pad = [(0, 0)] * rows.ndim
    pad[-2] = (rim_width, rim_width)
    padded = jnp.pad(rows, pad)
    summed = None
    for position in range(weights.shape[0]):
        displacement = LOWEST + position
        anchor = rim_width - displacement
        sliced = lax.slice_in_dim(padded, anchor, anchor + count, axis=rows.ndim - 2)
        weighted = sliced * weights[position]
        summed = weighted if summed is None else summed + weighted
    return summed


def left_block(count, sign):
    counter = np.arange(count)
    angle = (np.outer(counter, counter) % count) * (2.0 * np.pi / count)
    c = np.cos(angle)
    s = sign * np.sin(angle)
    return jnp.asarray(np.block([[c, -s], [s, c]]), jnp.float32)


def right_block(count, sign):
    counter = np.arange(count)
    angle = (np.outer(counter, counter) % count) * (2.0 * np.pi / count)
    c = np.cos(angle)
    s = sign * np.sin(angle)
    return jnp.asarray(np.block([[c, s], [-s, c]]), jnp.float32)


def twiddle(rows, cols, total, sign):
    angle = (np.outer(np.arange(rows), np.arange(cols)) % total) * (2.0 * np.pi / total)
    return jnp.asarray(np.stack([np.cos(angle), sign * np.sin(angle)]), jnp.float32)


def dot(a, b):
    return jnp.dot(a, b, precision=lax.Precision.HIGH, preferred_element_type=jnp.float32)


def forward_kernel(x_ref, w_ref, v_ref, t_ref, o_ref):
    nb, p_len, q_len = x_ref.shape[1], x_ref.shape[2], x_ref.shape[3]
    stacked = jnp.concatenate(
        [
            jnp.concatenate([x_ref[0, b] for b in range(nb)], axis=1),
            jnp.concatenate([x_ref[1, b] for b in range(nb)], axis=1),
        ],
        axis=0,
    )
    mid = dot(w_ref[...], stacked)
    tc = jnp.concatenate([t_ref[0]] * nb, axis=1)
    ts = jnp.concatenate([t_ref[1]] * nb, axis=1)
    mr = mid[:p_len]
    mi = mid[p_len:]
    tr = mr * tc - mi * ts
    ti = mi * tc + mr * ts
    turned = jnp.concatenate(
        [
            jnp.concatenate([tr[:, b * q_len : (b + 1) * q_len], ti[:, b * q_len : (b + 1) * q_len]], axis=1)
            for b in range(nb)
        ],
        axis=0,
    )
    out = dot(turned, v_ref[...])
    for b in range(nb):
        o_ref[0, b] = out[b * p_len : (b + 1) * p_len, :q_len]
        o_ref[1, b] = out[b * p_len : (b + 1) * p_len, q_len:]


def inverse_kernel(y_ref, v_ref, w_ref, t_ref, o_ref):
    nb, p_len, q_len = y_ref.shape[1], y_ref.shape[2], y_ref.shape[3]
    stacked = jnp.concatenate(
        [jnp.concatenate([y_ref[0, b], y_ref[1, b]], axis=1) for b in range(nb)], axis=0
    )
    mid = dot(stacked, v_ref[...])
    tc = jnp.concatenate([t_ref[0]] * nb, axis=0)
    ts = jnp.concatenate([t_ref[1]] * nb, axis=0)
    mr = mid[:, :q_len]
    mi = mid[:, q_len:]
    tr = mr * tc - mi * ts
    ti = mi * tc + mr * ts
    turned = jnp.concatenate(
        [
            jnp.concatenate([tr[b * p_len : (b + 1) * p_len] for b in range(nb)], axis=1),
            jnp.concatenate([ti[b * p_len : (b + 1) * p_len] for b in range(nb)], axis=1),
        ],
        axis=0,
    )
    out = dot(w_ref[...], turned)
    for b in range(nb):
        o_ref[0, b] = out[:p_len, b * q_len : (b + 1) * q_len]
        o_ref[1, b] = out[p_len:, b * q_len : (b + 1) * q_len]


def transpose_kernel(x_ref, o_ref):
    for b in range(x_ref.shape[0]):
        o_ref[b] = x_ref[b].T


def swap_minor(x):
    total, p_len, q_len = x.shape
    nb = block_count(total)
    return pl.pallas_call(
        transpose_kernel,
        out_shape=jax.ShapeDtypeStruct((total, q_len, p_len), x.dtype),
        grid=(total // nb,),
        in_specs=[pl.BlockSpec((nb, p_len, q_len), lambda i: (i, 0, 0))],
        out_specs=pl.BlockSpec((nb, q_len, p_len), lambda i: (i, 0, 0)),
        cost_estimate=pl.CostEstimate(flops=0, bytes_accessed=2 * x.size * 4, transcendentals=0),
    )(x)


def block_count(total):
    for nb in (8, 7, 6, 5, 4, 3, 2, 1):
        if total % nb == 0:
            return nb
    return 1


def run_transform(kernel, data, first, second, turn):
    _, total, p_len, q_len = data.shape
    nb = block_count(total)
    flops = 2 * 2 * total * (2 * p_len) * (2 * q_len) * (p_len + q_len) // 2
    return pl.pallas_call(
        kernel,
        out_shape=jax.ShapeDtypeStruct(data.shape, jnp.float32),
        grid=(total // nb,),
        in_specs=[
            pl.BlockSpec((2, nb, p_len, q_len), lambda i: (0, i, 0, 0)),
            pl.BlockSpec(first.shape, lambda i: (0, 0)),
            pl.BlockSpec(second.shape, lambda i: (0, 0)),
            pl.BlockSpec(turn.shape, lambda i: (0, 0, 0)),
        ],
        out_specs=pl.BlockSpec((2, nb, p_len, q_len), lambda i: (0, i, 0, 0)),
        cost_estimate=pl.CostEstimate(
            flops=flops, bytes_accessed=2 * data.size * 4, transcendentals=0
        ),
    )(data, first, second, turn)


def forward_transform(x, p_len, q_len):
    return run_transform(
        forward_kernel,
        x,
        left_block(p_len, -1.0),
        right_block(q_len, -1.0),
        twiddle(p_len, q_len, p_len * q_len, -1.0),
    )


def inverse_transform(y, p_len, q_len):
    return run_transform(
        inverse_kernel,
        y,
        right_block(q_len, 1.0),
        left_block(p_len, 1.0),
        twiddle(p_len, q_len, p_len * q_len, 1.0),
    )


def shrink(squares):
    magnitude = jnp.sqrt(squares)
    return jnp.maximum(magnitude - threshold, 0.0) / jnp.maximum(magnitude, threshold)


def body(
    observed,
    current_image,
    previous_image,
    doppler_phase,
    channel_ramp,
    range_offset,
    tap_index,
    kernel_table,
    group_of,
    calib_gain,
):
    lines = lax.axis_size("line")
    chans = lax.axis_size("chan")
    me = lax.axis_index("line")
    _, cl, rows, na = current_image.shape
    p_len = 128 if na % 128 == 0 else 1
    q_len = na // p_len

    levels = jnp.arange(G, dtype=jnp.int32)
    channel_gain = jnp.sum(
        (group_of[:, None] == levels[None, :]).astype(jnp.float32) * calib_gain[None, :], axis=1
    )

    momenta = momentum_weights()
    forward_pairs = [(i, i + 1) for i in range(lines - 1)]
    backward_pairs = [(i + 1, i) for i in range(lines - 1)]

    def edge_blend(lo, hi):
        cur = current_image[:, :, lo:hi]
        return cur + momenta[0] * (cur - previous_image[:, :, lo:hi])

    low = lax.ppermute(edge_blend(rows - HALO, rows), "line", forward_pairs)
    high = lax.ppermute(edge_blend(0, HALO), "line", backward_pairs)

    table = jnp.stack([tap_index, range_offset])
    table = jnp.broadcast_to(table[None], (lines,) + table.shape)
    table = lax.all_to_all(table, "line", split_axis=0, concat_axis=2, tiled=True)[0]

    earlier = previous_image.reshape(2, cl, rows, p_len, q_len)
    latest = current_image.reshape(2, cl, rows, p_len, q_len)
    blended = latest + momenta[0] * (latest - earlier)

    local_taps = tap_table(tap_index, kernel_table)
    local_weights = shift_weights(range_offset, local_taps)
    angles = doppler_phase[None, :, :] + channel_ramp[:, None, :]
    cos_a = jnp.cos(angles)
    sin_a = jnp.sin(angles)
    gain = channel_gain[:, None, None]
    back_r = gain * (cos_a * observed[0] + sin_a * observed[1])
    back_i = gain * (cos_a * observed[1] - sin_a * observed[0])
    data = adjoint_shift(jnp.stack([back_r, back_i]), local_weights)
    data = data * (step_length / math.sqrt(na))
    data, low, high, table = lax.optimization_barrier((data, low, high, table))
    data = data.reshape(2, cl, data.shape[2], data.shape[3] // p_len, p_len)
    data = lax.all_to_all(data, "line", split_axis=2, concat_axis=3, tiled=True)
    taps = tap_table(table[0], kernel_table)
    weights = shift_weights(table[1], taps)

    def spectral(v):
        return v.reshape(v.shape[:-1] + (q_len, p_len)).swapaxes(-1, -2)

    weights = spectral(weights)
    band = [
        spectral(sum(taps[:, k] * taps[:, k + e] for k in range(K - e))) for e in range(K)
    ]
    coef = (channel_gain * channel_gain) * (step_length / na)

    first = (me == 0)
    last = (me == lines - 1)

    def wgt(d):
        return weights[d - LOWEST]

    undo = None
    for iteration in range(ITERS):
        if iteration > 0:
            blended = latest + momenta[iteration] * (latest - earlier)
            low = lax.ppermute(blended[:, :, rows - HALO :], "line", forward_pairs)
            high = lax.ppermute(blended[:, :, :HALO], "line", backward_pairs)
            if iteration == ITERS - 1:
                prior = latest.reshape(current_image.shape)
                low, high, prior = lax.optimization_barrier((low, high, prior))
        elif ITERS == 1:
            prior = current_image
        own = forward_transform(blended.reshape(2, -1, p_len, q_len), p_len, q_len)
        own = own.reshape(2, cl, rows, p_len, q_len)
        rim = jnp.concatenate([low, high], axis=2).reshape(2, -1, p_len, q_len)
        rim = forward_transform(rim, p_len, q_len)
        rim = rim.reshape(2, cl, 2 * HALO, p_len, q_len)

        def at(r):
            if r < HALO:
                return rim[:, :, r]
            if r < HALO + rows:
                return own[:, :, r - HALO]
            return rim[:, :, r - rows]

        gram = []
        for r in range(rows):
            c = r + HALO
            acc = band[0] * at(c)
            for e in range(1, K):
                acc = acc + band[e] * (at(c - e) + at(c + e))
            gram.append(acc)
        low_fix = []
        for rr in range(K):
            acc = None
            for s in range(1, K + 1):
                if rr + s > OFFMAX + K // 2:
                    continue
                u = None
                for j in range(K):
                    if j + s > OFFMAX + K // 2:
                        continue
                    term = wgt(j + s) * at(HALO + j)
                    u = term if u is None else u + term
                term = wgt(rr + s) * u
                acc = term if acc is None else acc + term
            low_fix.append(acc)
        high_fix = []
        for tt in range(-(K - 2), 1):
            acc = None
            for s in range(1, K):
                if tt - s < LOWEST:
                    continue
                u = None
                for t in range(-(K - 2), 1):
                    if t - s < LOWEST:
                        continue
                    term = wgt(t - s) * at(HALO + rows - 1 + t)
                    u = term if u is None else u + term
                term = wgt(tt - s) * u
                acc = term if acc is None else acc + term
            high_fix.append(acc)
        for rr in range(K):
            gram[rr] = gram[rr] - jnp.where(first, low_fix[rr], 0.0)
        for idx, tt in enumerate(range(-(K - 2), 1)):
            r = rows - 1 + tt
            gram[r] = gram[r] - jnp.where(last, high_fix[idx], 0.0)
        gram = jnp.stack(gram, axis=2)
        resid = coef[None, :, None, None, None] * gram
        grad = inverse_transform(resid.reshape(2, -1, p_len, q_len), p_len, q_len)
        if undo is None:
            undo = swap_minor(data.reshape(-1, q_len, p_len))
            undo = inverse_transform(undo.reshape(2, -1, p_len, q_len), p_len, q_len)
            undo = undo.reshape(blended.shape)
        shifted = blended - grad.reshape(blended.shape) + undo
        squares = jnp.sum(shifted * shifted, axis=(0, 1))
        if chans == 2:
            squares = squares + lax.ppermute(squares, "chan", [(0, 1), (1, 0)])
        else:
            squares = lax.psum(squares, "chan")
        factor = shrink(squares)
        earlier = latest
        latest = shifted * factor[None, None]
    return (latest.reshape(current_image.shape), prior)


def solution(mesh):
    in_specs = (
        P(None, "chan", None, "line"),
        P(None, "chan", "line", None),
        P(None, "chan", "line", None),
        P(None, "line"),
        P("chan", "line"),
        P("line"),
        P("line"),
        P(),
        P("chan"),
        P(),
    )
    out_specs = (P(None, "chan", "line", None), P(None, "chan", "line", None))
    return jax.shard_map(body, mesh=mesh, in_specs=in_specs, out_specs=out_specs, check_vma=False)
```

```python
import math

import numpy as np
import jax
import jax.numpy as jnp
from jax import lax
from jax.sharding import PartitionSpec as P
from jax.experimental import pallas as pl

K = 4
Q = 16
OFFMAX = 2
G = 4
ITERS = 2
START_ITER = 8
HALO = K - 1

step_length = 0.25
threshold = 3.0


def momentum_weights():
    current = 1.0
    for counter in range(1, START_ITER):
        current = (1.0 + math.sqrt(1.0 + 4.0 * current * current)) / 2.0
    momenta = []
    for counter in range(ITERS):
        following = (1.0 + math.sqrt(1.0 + 4.0 * current * current)) / 2.0
        momenta.append((current - 1.0) / following)
        current = following
    return momenta


def tap_table(tap_index, kernel_table):
    levels = jnp.arange(Q, dtype=jnp.int32)
    onehot = (tap_index[:, None] == levels[None, :]).astype(jnp.float32)
    return jnp.dot(
        onehot, kernel_table, precision=lax.Precision.HIGHEST, preferred_element_type=jnp.float32
    )


def shift_weights(range_offset, tap_weights):
    stacked = []
    for displacement in range(-(OFFMAX + K // 2 - 1), OFFMAX + K // 2 + 1):
        summed = jnp.zeros(range_offset.shape, jnp.float32)
        for tap_number in range(K):
            matches = (range_offset + (tap_number - (K // 2 - 1)) == displacement).astype(
                jnp.float32
            )
            summed = summed + tap_weights[..., tap_number] * matches
        stacked.append(summed)
    return jnp.stack(stacked)


LOWEST = -(OFFMAX + K // 2 - 1)


def adjoint_shift(rows, weights):
    rim_width = OFFMAX + K // 2
    count = rows.shape[-2]
    pad = [(0, 0)] * rows.ndim
    pad[-2] = (rim_width, rim_width)
    padded = jnp.pad(rows, pad)
    summed = None
    for position in range(weights.shape[0]):
        displacement = LOWEST + position
        anchor = rim_width - displacement
        sliced = lax.slice_in_dim(padded, anchor, anchor + count, axis=rows.ndim - 2)
        weighted = sliced * weights[position]
        summed = weighted if summed is None else summed + weighted
    return summed


def left_block(count, sign):
    counter = np.arange(count)
    angle = (np.outer(counter, counter) % count) * (2.0 * np.pi / count)
    c = np.cos(angle)
    s = sign * np.sin(angle)
    return jnp.asarray(np.block([[c, -s], [s, c]]), jnp.float32)


def right_block(count, sign):
    counter = np.arange(count)
    angle = (np.outer(counter, counter) % count) * (2.0 * np.pi / count)
    c = np.cos(angle)
    s = sign * np.sin(angle)
    return jnp.asarray(np.block([[c, s], [-s, c]]), jnp.float32)


def twiddle(rows, cols, total, sign):
    angle = (np.outer(np.arange(rows), np.arange(cols)) % total) * (2.0 * np.pi / total)
    return jnp.asarray(np.stack([np.cos(angle), sign * np.sin(angle)]), jnp.float32)


def dot(a, b):
    return jnp.dot(a, b, precision=lax.Precision.HIGH, preferred_element_type=jnp.float32)


def forward_kernel(x_ref, w_ref, v_ref, t_ref, o_ref):
    nb, p_len, q_len = x_ref.shape[1], x_ref.shape[2], x_ref.shape[3]
    stacked = jnp.concatenate(
        [
            jnp.concatenate([x_ref[0, b] for b in range(nb)], axis=1),
            jnp.concatenate([x_ref[1, b] for b in range(nb)], axis=1),
        ],
        axis=0,
    )
    mid = dot(w_ref[...], stacked)
    tc = jnp.concatenate([t_ref[0]] * nb, axis=1)
    ts = jnp.concatenate([t_ref[1]] * nb, axis=1)
    mr = mid[:p_len]
    mi = mid[p_len:]
    tr = mr * tc - mi * ts
    ti = mi * tc + mr * ts
    turned = jnp.concatenate(
        [
            jnp.concatenate([tr[:, b * q_len : (b + 1) * q_len], ti[:, b * q_len : (b + 1) * q_len]], axis=1)
            for b in range(nb)
        ],
        axis=0,
    )
    out = dot(turned, v_ref[...])
    for b in range(nb):
        o_ref[0, b] = out[b * p_len : (b + 1) * p_len, :q_len]
        o_ref[1, b] = out[b * p_len : (b + 1) * p_len, q_len:]


def inverse_kernel(y_ref, v_ref, w_ref, t_ref, o_ref):
    nb, p_len, q_len = y_ref.shape[1], y_ref.shape[2], y_ref.shape[3]
    stacked = jnp.concatenate(
        [jnp.concatenate([y_ref[0, b], y_ref[1, b]], axis=1) for b in range(nb)], axis=0
    )
    mid = dot(stacked, v_ref[...])
    tc = jnp.concatenate([t_ref[0]] * nb, axis=0)
    ts = jnp.concatenate([t_ref[1]] * nb, axis=0)
    mr = mid[:, :q_len]
    mi = mid[:, q_len:]
    tr = mr * tc - mi * ts
    ti = mi * tc + mr * ts
    turned = jnp.concatenate(
        [
            jnp.concatenate([tr[b * p_len : (b + 1) * p_len] for b in range(nb)], axis=1),
            jnp.concatenate([ti[b * p_len : (b + 1) * p_len] for b in range(nb)], axis=1),
        ],
        axis=0,
    )
    out = dot(w_ref[...], turned)
    for b in range(nb):
        o_ref[0, b] = out[:p_len, b * q_len : (b + 1) * q_len]
        o_ref[1, b] = out[p_len:, b * q_len : (b + 1) * q_len]


def transpose_kernel(x_ref, o_ref):
    for b in range(x_ref.shape[0]):
        o_ref[b] = x_ref[b].T


def swap_minor(x):
    total, p_len, q_len = x.shape
    nb = block_count(total)
    return pl.pallas_call(
        transpose_kernel,
        out_shape=jax.ShapeDtypeStruct((total, q_len, p_len), x.dtype),
        grid=(total // nb,),
        in_specs=[pl.BlockSpec((nb, p_len, q_len), lambda i: (i, 0, 0))],
        out_specs=pl.BlockSpec((nb, q_len, p_len), lambda i: (i, 0, 0)),
        cost_estimate=pl.CostEstimate(flops=0, bytes_accessed=2 * x.size * 4, transcendentals=0),
    )(x)


def block_count(total):
    for nb in (8, 7, 6, 5, 4, 3, 2, 1):
        if total % nb == 0:
            return nb
    return 1


def run_transform(kernel, data, first, second, turn):
    _, total, p_len, q_len = data.shape
    nb = block_count(total)
    flops = 2 * 2 * total * (2 * p_len) * (2 * q_len) * (p_len + q_len) // 2
    return pl.pallas_call(
        kernel,
        out_shape=jax.ShapeDtypeStruct(data.shape, jnp.float32),
        grid=(total // nb,),
        in_specs=[
            pl.BlockSpec((2, nb, p_len, q_len), lambda i: (0, i, 0, 0)),
            pl.BlockSpec(first.shape, lambda i: (0, 0)),
            pl.BlockSpec(second.shape, lambda i: (0, 0)),
            pl.BlockSpec(turn.shape, lambda i: (0, 0, 0)),
        ],
        out_specs=pl.BlockSpec((2, nb, p_len, q_len), lambda i: (0, i, 0, 0)),
        cost_estimate=pl.CostEstimate(
            flops=flops, bytes_accessed=2 * data.size * 4, transcendentals=0
        ),
    )(data, first, second, turn)


def forward_transform(x, p_len, q_len):
    return run_transform(
        forward_kernel,
        x,
        left_block(p_len, -1.0),
        right_block(q_len, -1.0),
        twiddle(p_len, q_len, p_len * q_len, -1.0),
    )


def inverse_transform(y, p_len, q_len):
    return run_transform(
        inverse_kernel,
        y,
        right_block(q_len, 1.0),
        left_block(p_len, 1.0),
        twiddle(p_len, q_len, p_len * q_len, 1.0),
    )


def shrink(squares):
    magnitude = jnp.sqrt(squares)
    return jnp.maximum(magnitude - threshold, 0.0) / jnp.maximum(magnitude, threshold)


def body(
    observed,
    current_image,
    previous_image,
    doppler_phase,
    channel_ramp,
    range_offset,
    tap_index,
    kernel_table,
    group_of,
    calib_gain,
):
    lines = lax.axis_size("line")
    chans = lax.axis_size("chan")
    me = lax.axis_index("line")
    _, cl, rows, na = current_image.shape
    p_len = 128 if na % 128 == 0 else 1
    q_len = na // p_len

    levels = jnp.arange(G, dtype=jnp.int32)
    channel_gain = jnp.sum(
        (group_of[:, None] == levels[None, :]).astype(jnp.float32) * calib_gain[None, :], axis=1
    )

    momenta = momentum_weights()
    forward_pairs = [(i, i + 1) for i in range(lines - 1)]
    backward_pairs = [(i + 1, i) for i in range(lines - 1)]

    earlier = previous_image.reshape(2, cl, rows, p_len, q_len)
    latest = current_image.reshape(2, cl, rows, p_len, q_len)

    def edge_blend(lo, hi):
        cur = latest[:, :, lo:hi]
        return cur + momenta[0] * (cur - earlier[:, :, lo:hi])

    low = lax.ppermute(edge_blend(rows - HALO, rows), "line", forward_pairs)
    high = lax.ppermute(edge_blend(0, HALO), "line", backward_pairs)

    table = jnp.stack([tap_index, range_offset])
    table = jnp.broadcast_to(table[None], (lines,) + table.shape)
    table = lax.all_to_all(table, "line", split_axis=0, concat_axis=2, tiled=True)[0]

    blended = latest + momenta[0] * (latest - earlier)

    local_taps = tap_table(tap_index, kernel_table)
    local_weights = shift_weights(range_offset, local_taps)
    angles = doppler_phase[None, :, :] + channel_ramp[:, None, :]
    cos_a = jnp.cos(angles)
    sin_a = jnp.sin(angles)
    gain = channel_gain[:, None, None]
    back_r = gain * (cos_a * observed[0] + sin_a * observed[1])
    back_i = gain * (cos_a * observed[1] - sin_a * observed[0])
    data = adjoint_shift(jnp.stack([back_r, back_i]), local_weights)
    data = data * (step_length / math.sqrt(na))
    data, low, high, table = lax.optimization_barrier((data, low, high, table))
    data = data.reshape(2, cl, data.shape[2], data.shape[3] // p_len, p_len)
    data = lax.all_to_all(data, "line", split_axis=2, concat_axis=3, tiled=True)
    taps = tap_table(table[0], kernel_table)
    weights = shift_weights(table[1], taps)

    def spectral(v):
        return v.reshape(v.shape[:-1] + (q_len, p_len)).swapaxes(-1, -2)

    weights = spectral(weights)
    band = [
        spectral(sum(taps[:, k] * taps[:, k + e] for k in range(K - e))) for e in range(K)
    ]
    coef = (channel_gain * channel_gain) * (step_length / na)

    first = (me == 0)
    last = (me == lines - 1)

    def wgt(d):
        return weights[d - LOWEST]

    undo = None
    for iteration in range(ITERS):
        if iteration > 0:
            blended = latest + momenta[iteration] * (latest - earlier)
            low = lax.ppermute(blended[:, :, rows - HALO :], "line", forward_pairs)
            high = lax.ppermute(blended[:, :, :HALO], "line", backward_pairs)
            if iteration == ITERS - 1:
                prior = latest.reshape(current_image.shape)
                low, high, prior = lax.optimization_barrier((low, high, prior))
        elif ITERS == 1:
            prior = current_image
        own = forward_transform(blended.reshape(2, -1, p_len, q_len), p_len, q_len)
        own = own.reshape(2, cl, rows, p_len, q_len)
        rim = jnp.concatenate([low, high], axis=2).reshape(2, -1, p_len, q_len)
        rim = forward_transform(rim, p_len, q_len)
        rim = rim.reshape(2, cl, 2 * HALO, p_len, q_len)

        def at(r):
            if r < HALO:
                return rim[:, :, r]
            if r < HALO + rows:
                return own[:, :, r - HALO]
            return rim[:, :, r - rows]

        gram = []
        for r in range(rows):
            c = r + HALO
            acc = band[0] * at(c)
            for e in range(1, K):
                acc = acc + band[e] * (at(c - e) + at(c + e))
            gram.append(acc)
        low_fix = []
        for rr in range(K):
            acc = None
            for s in range(1, K + 1):
                if rr + s > OFFMAX + K // 2:
                    continue
                u = None
                for j in range(K):
                    if j + s > OFFMAX + K // 2:
                        continue
                    term = wgt(j + s) * at(HALO + j)
                    u = term if u is None else u + term
                term = wgt(rr + s) * u
                acc = term if acc is None else acc + term
            low_fix.append(acc)
        high_fix = []
        for tt in range(-(K - 2), 1):
            acc = None
            for s in range(1, K):
                if tt - s < LOWEST:
                    continue
                u = None
                for t in range(-(K - 2), 1):
                    if t - s < LOWEST:
                        continue
                    term = wgt(t - s) * at(HALO + rows - 1 + t)
                    u = term if u is None else u + term
                term = wgt(tt - s) * u
                acc = term if acc is None else acc + term
            high_fix.append(acc)
        for rr in range(K):
            gram[rr] = gram[rr] - jnp.where(first, low_fix[rr], 0.0)
        for idx, tt in enumerate(range(-(K - 2), 1)):
            r = rows - 1 + tt
            gram[r] = gram[r] - jnp.where(last, high_fix[idx], 0.0)
        gram = jnp.stack(gram, axis=2)
        resid = coef[None, :, None, None, None] * gram
        grad = inverse_transform(resid.reshape(2, -1, p_len, q_len), p_len, q_len)
        if undo is None:
            undo = swap_minor(data.reshape(-1, q_len, p_len))
            undo = inverse_transform(undo.reshape(2, -1, p_len, q_len), p_len, q_len)
            undo = undo.reshape(blended.shape)
        shifted = blended - grad.reshape(blended.shape) + undo
        squares = jnp.sum(shifted * shifted, axis=(0, 1))
        if chans == 2:
            squares = squares + lax.ppermute(squares, "chan", [(0, 1), (1, 0)])
        else:
            squares = lax.psum(squares, "chan")
        factor = shrink(squares)
        earlier = latest
        latest = shifted * factor[None, None]
    return (latest.reshape(current_image.shape), prior)


def solution(mesh):
    in_specs = (
        P(None, "chan", None, "line"),
        P(None, "chan", "line", None),
        P(None, "chan", "line", None),
        P(None, "line"),
        P("chan", "line"),
        P("line"),
        P("line"),
        P(),
        P("chan"),
        P(),
    )
    out_specs = (P(None, "chan", "line", None), P(None, "chan", "line", None))
    return jax.shard_map(body, mesh=mesh, in_specs=in_specs, out_specs=out_specs, check_vma=False)
```

```python
import math

import numpy as np
import jax
import jax.numpy as jnp
from jax import lax
from jax.sharding import PartitionSpec as P
from jax.experimental import pallas as pl

K = 4
Q = 16
OFFMAX = 2
G = 4
ITERS = 2
START_ITER = 8
HALO = K - 1

step_length = 0.25
threshold = 3.0


def momentum_weights():
    current = 1.0
    for counter in range(1, START_ITER):
        current = (1.0 + math.sqrt(1.0 + 4.0 * current * current)) / 2.0
    momenta = []
    for counter in range(ITERS):
        following = (1.0 + math.sqrt(1.0 + 4.0 * current * current)) / 2.0
        momenta.append((current - 1.0) / following)
        current = following
    return momenta


def tap_table(tap_index, kernel_table):
    levels = jnp.arange(Q, dtype=jnp.int32)
    onehot = (tap_index[:, None] == levels[None, :]).astype(jnp.float32)
    return jnp.dot(
        onehot, kernel_table, precision=lax.Precision.HIGHEST, preferred_element_type=jnp.float32
    )


def shift_weights(range_offset, tap_weights):
    stacked = []
    for displacement in range(-(OFFMAX + K // 2 - 1), OFFMAX + K // 2 + 1):
        summed = jnp.zeros(range_offset.shape, jnp.float32)
        for tap_number in range(K):
            matches = (range_offset + (tap_number - (K // 2 - 1)) == displacement).astype(
                jnp.float32
            )
            summed = summed + tap_weights[..., tap_number] * matches
        stacked.append(summed)
    return jnp.stack(stacked)


LOWEST = -(OFFMAX + K // 2 - 1)


def adjoint_shift(rows, weights):
    rim_width = OFFMAX + K // 2
    count = rows.shape[-2]
    pad = [(0, 0)] * rows.ndim
    pad[-2] = (rim_width, rim_width)
    padded = jnp.pad(rows, pad)
    summed = None
    for position in range(weights.shape[0]):
        displacement = LOWEST + position
        anchor = rim_width - displacement
        sliced = lax.slice_in_dim(padded, anchor, anchor + count, axis=rows.ndim - 2)
        weighted = sliced * weights[position]
        summed = weighted if summed is None else summed + weighted
    return summed


def left_block(count, sign):
    counter = np.arange(count)
    angle = (np.outer(counter, counter) % count) * (2.0 * np.pi / count)
    c = np.cos(angle)
    s = sign * np.sin(angle)
    return jnp.asarray(np.block([[c, -s], [s, c]]), jnp.float32)


def right_block(count, sign):
    counter = np.arange(count)
    angle = (np.outer(counter, counter) % count) * (2.0 * np.pi / count)
    c = np.cos(angle)
    s = sign * np.sin(angle)
    return jnp.asarray(np.block([[c, s], [-s, c]]), jnp.float32)


def twiddle(rows, cols, total, sign):
    angle = (np.outer(np.arange(rows), np.arange(cols)) % total) * (2.0 * np.pi / total)
    return jnp.asarray(np.stack([np.cos(angle), sign * np.sin(angle)]), jnp.float32)


def dot(a, b):
    return jnp.dot(a, b, precision=lax.Precision.HIGH, preferred_element_type=jnp.float32)


def forward_kernel(x_ref, w_ref, v_ref, t_ref, o_ref):
    nb, p_len, q_len = x_ref.shape[1], x_ref.shape[2], x_ref.shape[3]
    stacked = jnp.concatenate(
        [
            jnp.concatenate([x_ref[0, b] for b in range(nb)], axis=1),
            jnp.concatenate([x_ref[1, b] for b in range(nb)], axis=1),
        ],
        axis=0,
    )
    mid = dot(w_ref[...], stacked)
    tc = jnp.concatenate([t_ref[0]] * nb, axis=1)
    ts = jnp.concatenate([t_ref[1]] * nb, axis=1)
    mr = mid[:p_len]
    mi = mid[p_len:]
    tr = mr * tc - mi * ts
    ti = mi * tc + mr * ts
    turned = jnp.concatenate(
        [
            jnp.concatenate([tr[:, b * q_len : (b + 1) * q_len], ti[:, b * q_len : (b + 1) * q_len]], axis=1)
            for b in range(nb)
        ],
        axis=0,
    )
    out = dot(turned, v_ref[...])
    for b in range(nb):
        o_ref[0, b] = out[b * p_len : (b + 1) * p_len, :q_len]
        o_ref[1, b] = out[b * p_len : (b + 1) * p_len, q_len:]


def inverse_kernel(y_ref, v_ref, w_ref, t_ref, o_ref):
    nb, p_len, q_len = y_ref.shape[1], y_ref.shape[2], y_ref.shape[3]
    stacked = jnp.concatenate(
        [jnp.concatenate([y_ref[0, b], y_ref[1, b]], axis=1) for b in range(nb)], axis=0
    )
    mid = dot(stacked, v_ref[...])
    tc = jnp.concatenate([t_ref[0]] * nb, axis=0)
    ts = jnp.concatenate([t_ref[1]] * nb, axis=0)
    mr = mid[:, :q_len]
    mi = mid[:, q_len:]
    tr = mr * tc - mi * ts
    ti = mi * tc + mr * ts
    turned = jnp.concatenate(
        [
            jnp.concatenate([tr[b * p_len : (b + 1) * p_len] for b in range(nb)], axis=1),
            jnp.concatenate([ti[b * p_len : (b + 1) * p_len] for b in range(nb)], axis=1),
        ],
        axis=0,
    )
    out = dot(w_ref[...], turned)
    for b in range(nb):
        o_ref[0, b] = out[:p_len, b * q_len : (b + 1) * q_len]
        o_ref[1, b] = out[p_len:, b * q_len : (b + 1) * q_len]


def transpose_kernel(x_ref, o_ref):
    for b in range(x_ref.shape[0]):
        o_ref[b] = x_ref[b].T


def swap_minor(x):
    total, p_len, q_len = x.shape
    nb = block_count(total)
    return pl.pallas_call(
        transpose_kernel,
        out_shape=jax.ShapeDtypeStruct((total, q_len, p_len), x.dtype),
        grid=(total // nb,),
        in_specs=[pl.BlockSpec((nb, p_len, q_len), lambda i: (i, 0, 0))],
        out_specs=pl.BlockSpec((nb, q_len, p_len), lambda i: (i, 0, 0)),
        cost_estimate=pl.CostEstimate(flops=0, bytes_accessed=2 * x.size * 4, transcendentals=0),
    )(x)


def block_count(total):
    for nb in (8, 7, 6, 5, 4, 3, 2, 1):
        if total % nb == 0:
            return nb
    return 1


def run_transform(kernel, data, first, second, turn):
    _, total, p_len, q_len = data.shape
    nb = block_count(total)
    flops = 2 * 2 * total * (2 * p_len) * (2 * q_len) * (p_len + q_len) // 2
    return pl.pallas_call(
        kernel,
        out_shape=jax.ShapeDtypeStruct(data.shape, jnp.float32),
        grid=(total // nb,),
        in_specs=[
            pl.BlockSpec((2, nb, p_len, q_len), lambda i: (0, i, 0, 0)),
            pl.BlockSpec(first.shape, lambda i: (0, 0)),
            pl.BlockSpec(second.shape, lambda i: (0, 0)),
            pl.BlockSpec(turn.shape, lambda i: (0, 0, 0)),
        ],
        out_specs=pl.BlockSpec((2, nb, p_len, q_len), lambda i: (0, i, 0, 0)),
        cost_estimate=pl.CostEstimate(
            flops=flops, bytes_accessed=2 * data.size * 4, transcendentals=0
        ),
    )(data, first, second, turn)


def forward_transform(x, p_len, q_len):
    return run_transform(
        forward_kernel,
        x,
        left_block(p_len, -1.0),
        right_block(q_len, -1.0),
        twiddle(p_len, q_len, p_len * q_len, -1.0),
    )


def inverse_transform(y, p_len, q_len):
    return run_transform(
        inverse_kernel,
        y,
        right_block(q_len, 1.0),
        left_block(p_len, 1.0),
        twiddle(p_len, q_len, p_len * q_len, 1.0),
    )


def shrink(squares):
    magnitude = jnp.sqrt(squares)
    return jnp.maximum(magnitude - threshold, 0.0) / jnp.maximum(magnitude, threshold)


def body(
    observed,
    current_image,
    previous_image,
    doppler_phase,
    channel_ramp,
    range_offset,
    tap_index,
    kernel_table,
    group_of,
    calib_gain,
):
    lines = lax.axis_size("line")
    chans = lax.axis_size("chan")
    me = lax.axis_index("line")
    _, cl, rows, na = current_image.shape
    p_len = 128 if na % 128 == 0 else 1
    q_len = na // p_len

    levels = jnp.arange(G, dtype=jnp.int32)
    channel_gain = jnp.sum(
        (group_of[:, None] == levels[None, :]).astype(jnp.float32) * calib_gain[None, :], axis=1
    )

    momenta = momentum_weights()
    forward_pairs = [(i, i + 1) for i in range(lines - 1)]
    backward_pairs = [(i + 1, i) for i in range(lines - 1)]

    earlier = previous_image.reshape(2, cl, rows, p_len, q_len)
    latest = current_image.reshape(2, cl, rows, p_len, q_len)

    def edge_blend(lo, hi):
        cur = latest[:, :, lo:hi]
        return cur + momenta[0] * (cur - earlier[:, :, lo:hi])

    low = lax.ppermute(edge_blend(rows - HALO, rows), "line", forward_pairs)
    high = lax.ppermute(edge_blend(0, HALO), "line", backward_pairs)

    table = jnp.stack([tap_index, range_offset])
    table = jnp.broadcast_to(table[None], (lines,) + table.shape)
    table = lax.all_to_all(table, "line", split_axis=0, concat_axis=2, tiled=True)[0]

    blended = latest + momenta[0] * (latest - earlier)

    local_taps = tap_table(tap_index, kernel_table)
    local_weights = shift_weights(range_offset, local_taps)
    angles = doppler_phase[None, :, :] + channel_ramp[:, None, :]
    cos_a = jnp.cos(angles)
    sin_a = jnp.sin(angles)
    gain = channel_gain[:, None, None]
    back_r = gain * (cos_a * observed[0] + sin_a * observed[1])
    back_i = gain * (cos_a * observed[1] - sin_a * observed[0])
    data = adjoint_shift(jnp.stack([back_r, back_i]), local_weights)
    data = data * (step_length / math.sqrt(na))
    data, low, high, table = lax.optimization_barrier((data, low, high, table))
    data = data.reshape(2, cl, data.shape[2], data.shape[3] // p_len, p_len)
    halves = 2 if cl % 2 == 0 else 1
    pieces = []
    for h in range(halves):
        piece = data[:, h * cl // halves : (h + 1) * cl // halves]
        if pieces:
            piece, pieces[-1] = lax.optimization_barrier((piece, pieces[-1]))
        pieces.append(lax.all_to_all(piece, "line", split_axis=2, concat_axis=3, tiled=True))
    taps = tap_table(table[0], kernel_table)
    weights = shift_weights(table[1], taps)

    def spectral(v):
        return v.reshape(v.shape[:-1] + (q_len, p_len)).swapaxes(-1, -2)

    weights = spectral(weights)
    band = [
        spectral(sum(taps[:, k] * taps[:, k + e] for k in range(K - e))) for e in range(K)
    ]
    coef = (channel_gain * channel_gain) * (step_length / na)

    first = (me == 0)
    last = (me == lines - 1)

    def wgt(d):
        return weights[d - LOWEST]

    undo = None
    for iteration in range(ITERS):
        if iteration > 0:
            blended = latest + momenta[iteration] * (latest - earlier)
            low = lax.ppermute(blended[:, :, rows - HALO :], "line", forward_pairs)
            high = lax.ppermute(blended[:, :, :HALO], "line", backward_pairs)
            if iteration == ITERS - 1:
                prior = latest.reshape(current_image.shape)
                low, high, prior = lax.optimization_barrier((low, high, prior))
        elif ITERS == 1:
            prior = current_image
        own = forward_transform(blended.reshape(2, -1, p_len, q_len), p_len, q_len)
        own = own.reshape(2, cl, rows, p_len, q_len)
        rim = jnp.concatenate([low, high], axis=2).reshape(2, -1, p_len, q_len)
        rim = forward_transform(rim, p_len, q_len)
        rim = rim.reshape(2, cl, 2 * HALO, p_len, q_len)

        def at(r):
            if r < HALO:
                return rim[:, :, r]
            if r < HALO + rows:
                return own[:, :, r - HALO]
            return rim[:, :, r - rows]

        gram = []
        for r in range(rows):
            c = r + HALO
            acc = band[0] * at(c)
            for e in range(1, K):
                acc = acc + band[e] * (at(c - e) + at(c + e))
            gram.append(acc)
        low_fix = []
        for rr in range(K):
            acc = None
            for s in range(1, K + 1):
                if rr + s > OFFMAX + K // 2:
                    continue
                u = None
                for j in range(K):
                    if j + s > OFFMAX + K // 2:
                        continue
                    term = wgt(j + s) * at(HALO + j)
                    u = term if u is None else u + term
                term = wgt(rr + s) * u
                acc = term if acc is None else acc + term
            low_fix.append(acc)
        high_fix = []
        for tt in range(-(K - 2), 1):
            acc = None
            for s in range(1, K):
                if tt - s < LOWEST:
                    continue
                u = None
                for t in range(-(K - 2), 1):
                    if t - s < LOWEST:
                        continue
                    term = wgt(t - s) * at(HALO + rows - 1 + t)
                    u = term if u is None else u + term
                term = wgt(tt - s) * u
                acc = term if acc is None else acc + term
            high_fix.append(acc)
        for rr in range(K):
            gram[rr] = gram[rr] - jnp.where(first, low_fix[rr], 0.0)
        for idx, tt in enumerate(range(-(K - 2), 1)):
            r = rows - 1 + tt
            gram[r] = gram[r] - jnp.where(last, high_fix[idx], 0.0)
        gram = jnp.stack(gram, axis=2)
        resid = coef[None, :, None, None, None] * gram
        grad = inverse_transform(resid.reshape(2, -1, p_len, q_len), p_len, q_len)
        if undo is None:
            undo = []
            for piece in pieces:
                part = swap_minor(piece.reshape(-1, q_len, p_len))
                part = inverse_transform(part.reshape(2, -1, p_len, q_len), p_len, q_len)
                undo.append(part.reshape(2, -1, rows, p_len, q_len))
            undo = jnp.concatenate(undo, axis=1)
        shifted = blended - grad.reshape(blended.shape) + undo
        squares = jnp.sum(shifted * shifted, axis=(0, 1))
        if chans == 2:
            squares = squares + lax.ppermute(squares, "chan", [(0, 1), (1, 0)])
        else:
            squares = lax.psum(squares, "chan")
        factor = shrink(squares)
        earlier = latest
        latest = shifted * factor[None, None]
    return (latest.reshape(current_image.shape), prior)


def solution(mesh):
    in_specs = (
        P(None, "chan", None, "line"),
        P(None, "chan", "line", None),
        P(None, "chan", "line", None),
        P(None, "line"),
        P("chan", "line"),
        P("line"),
        P("line"),
        P(),
        P("chan"),
        P(),
    )
    out_specs = (P(None, "chan", "line", None), P(None, "chan", "line", None))
    return jax.shard_map(body, mesh=mesh, in_specs=in_specs, out_specs=out_specs, check_vma=False)
```

```python
import math

import numpy as np
import jax
import jax.numpy as jnp
from jax import lax
from jax.sharding import PartitionSpec as P
from jax.experimental import pallas as pl

K = 4
Q = 16
OFFMAX = 2
G = 4
ITERS = 2
START_ITER = 8
HALO = K - 1

step_length = 0.25
threshold = 3.0


def momentum_weights():
    current = 1.0
    for counter in range(1, START_ITER):
        current = (1.0 + math.sqrt(1.0 + 4.0 * current * current)) / 2.0
    momenta = []
    for counter in range(ITERS):
        following = (1.0 + math.sqrt(1.0 + 4.0 * current * current)) / 2.0
        momenta.append((current - 1.0) / following)
        current = following
    return momenta


def tap_table(tap_index, kernel_table):
    levels = jnp.arange(Q, dtype=jnp.int32)
    onehot = (tap_index[:, None] == levels[None, :]).astype(jnp.float32)
    return jnp.dot(
        onehot, kernel_table, precision=lax.Precision.HIGHEST, preferred_element_type=jnp.float32
    )


def shift_weights(range_offset, tap_weights):
    stacked = []
    for displacement in range(-(OFFMAX + K // 2 - 1), OFFMAX + K // 2 + 1):
        summed = jnp.zeros(range_offset.shape, jnp.float32)
        for tap_number in range(K):
            matches = (range_offset + (tap_number - (K // 2 - 1)) == displacement).astype(
                jnp.float32
            )
            summed = summed + tap_weights[..., tap_number] * matches
        stacked.append(summed)
    return jnp.stack(stacked)


LOWEST = -(OFFMAX + K // 2 - 1)


def adjoint_shift(rows, weights):
    rim_width = OFFMAX + K // 2
    count = rows.shape[-2]
    pad = [(0, 0)] * rows.ndim
    pad[-2] = (rim_width, rim_width)
    padded = jnp.pad(rows, pad)
    summed = None
    for position in range(weights.shape[0]):
        displacement = LOWEST + position
        anchor = rim_width - displacement
        sliced = lax.slice_in_dim(padded, anchor, anchor + count, axis=rows.ndim - 2)
        weighted = sliced * weights[position]
        summed = weighted if summed is None else summed + weighted
    return summed


def left_block(count, sign):
    counter = np.arange(count)
    angle = (np.outer(counter, counter) % count) * (2.0 * np.pi / count)
    c = np.cos(angle)
    s = sign * np.sin(angle)
    return jnp.asarray(np.block([[c, -s], [s, c]]), jnp.float32)


def right_block(count, sign):
    counter = np.arange(count)
    angle = (np.outer(counter, counter) % count) * (2.0 * np.pi / count)
    c = np.cos(angle)
    s = sign * np.sin(angle)
    return jnp.asarray(np.block([[c, s], [-s, c]]), jnp.float32)


def twiddle(rows, cols, total, sign):
    angle = (np.outer(np.arange(rows), np.arange(cols)) % total) * (2.0 * np.pi / total)
    return jnp.asarray(np.stack([np.cos(angle), sign * np.sin(angle)]), jnp.float32)


def dot(a, b):
    return jnp.dot(a, b, precision=lax.Precision.HIGH, preferred_element_type=jnp.float32)


def forward_kernel(x_ref, w_ref, v_ref, t_ref, o_ref):
    nb, p_len, q_len = x_ref.shape[1], x_ref.shape[2], x_ref.shape[3]
    stacked = jnp.concatenate(
        [
            jnp.concatenate([x_ref[0, b] for b in range(nb)], axis=1),
            jnp.concatenate([x_ref[1, b] for b in range(nb)], axis=1),
        ],
        axis=0,
    )
    mid = dot(w_ref[...], stacked)
    tc = jnp.concatenate([t_ref[0]] * nb, axis=1)
    ts = jnp.concatenate([t_ref[1]] * nb, axis=1)
    mr = mid[:p_len]
    mi = mid[p_len:]
    tr = mr * tc - mi * ts
    ti = mi * tc + mr * ts
    turned = jnp.concatenate(
        [
            jnp.concatenate([tr[:, b * q_len : (b + 1) * q_len], ti[:, b * q_len : (b + 1) * q_len]], axis=1)
            for b in range(nb)
        ],
        axis=0,
    )
    out = dot(turned, v_ref[...])
    for b in range(nb):
        o_ref[0, b] = out[b * p_len : (b + 1) * p_len, :q_len]
        o_ref[1, b] = out[b * p_len : (b + 1) * p_len, q_len:]


def inverse_kernel(y_ref, v_ref, w_ref, t_ref, o_ref):
    nb, p_len, q_len = y_ref.shape[1], y_ref.shape[2], y_ref.shape[3]
    stacked = jnp.concatenate(
        [jnp.concatenate([y_ref[0, b], y_ref[1, b]], axis=1) for b in range(nb)], axis=0
    )
    mid = dot(stacked, v_ref[...])
    tc = jnp.concatenate([t_ref[0]] * nb, axis=0)
    ts = jnp.concatenate([t_ref[1]] * nb, axis=0)
    mr = mid[:, :q_len]
    mi = mid[:, q_len:]
    tr = mr * tc - mi * ts
    ti = mi * tc + mr * ts
    turned = jnp.concatenate(
        [
            jnp.concatenate([tr[b * p_len : (b + 1) * p_len] for b in range(nb)], axis=1),
            jnp.concatenate([ti[b * p_len : (b + 1) * p_len] for b in range(nb)], axis=1),
        ],
        axis=0,
    )
    out = dot(w_ref[...], turned)
    for b in range(nb):
        o_ref[0, b] = out[:p_len, b * q_len : (b + 1) * q_len]
        o_ref[1, b] = out[p_len:, b * q_len : (b + 1) * q_len]


def transpose_kernel(x_ref, o_ref):
    for b in range(x_ref.shape[0]):
        o_ref[b] = x_ref[b].T


def swap_minor(x):
    total, p_len, q_len = x.shape
    nb = block_count(total)
    return pl.pallas_call(
        transpose_kernel,
        out_shape=jax.ShapeDtypeStruct((total, q_len, p_len), x.dtype),
        grid=(total // nb,),
        in_specs=[pl.BlockSpec((nb, p_len, q_len), lambda i: (i, 0, 0))],
        out_specs=pl.BlockSpec((nb, q_len, p_len), lambda i: (i, 0, 0)),
        cost_estimate=pl.CostEstimate(flops=0, bytes_accessed=2 * x.size * 4, transcendentals=0),
    )(x)


def block_count(total):
    for nb in (16, 8, 7, 6, 5, 4, 3, 2, 1):
        if total % nb == 0:
            return nb
    return 1


def run_transform(kernel, data, first, second, turn):
    _, total, p_len, q_len = data.shape
    nb = block_count(total)
    flops = 2 * 2 * total * (2 * p_len) * (2 * q_len) * (p_len + q_len) // 2
    return pl.pallas_call(
        kernel,
        out_shape=jax.ShapeDtypeStruct(data.shape, jnp.float32),
        grid=(total // nb,),
        in_specs=[
            pl.BlockSpec((2, nb, p_len, q_len), lambda i: (0, i, 0, 0)),
            pl.BlockSpec(first.shape, lambda i: (0, 0)),
            pl.BlockSpec(second.shape, lambda i: (0, 0)),
            pl.BlockSpec(turn.shape, lambda i: (0, 0, 0)),
        ],
        out_specs=pl.BlockSpec((2, nb, p_len, q_len), lambda i: (0, i, 0, 0)),
        cost_estimate=pl.CostEstimate(
            flops=flops, bytes_accessed=2 * data.size * 4, transcendentals=0
        ),
    )(data, first, second, turn)


def forward_transform(x, p_len, q_len):
    return run_transform(
        forward_kernel,
        x,
        left_block(p_len, -1.0),
        right_block(q_len, -1.0),
        twiddle(p_len, q_len, p_len * q_len, -1.0),
    )


def inverse_transform(y, p_len, q_len):
    return run_transform(
        inverse_kernel,
        y,
        right_block(q_len, 1.0),
        left_block(p_len, 1.0),
        twiddle(p_len, q_len, p_len * q_len, 1.0),
    )


def shrink(squares):
    magnitude = jnp.sqrt(squares)
    return jnp.maximum(magnitude - threshold, 0.0) / jnp.maximum(magnitude, threshold)


def body(
    observed,
    current_image,
    previous_image,
    doppler_phase,
    channel_ramp,
    range_offset,
    tap_index,
    kernel_table,
    group_of,
    calib_gain,
):
    lines = lax.axis_size("line")
    chans = lax.axis_size("chan")
    me = lax.axis_index("line")
    _, cl, rows, na = current_image.shape
    p_len = 128 if na % 128 == 0 else 1
    q_len = na // p_len

    levels = jnp.arange(G, dtype=jnp.int32)
    channel_gain = jnp.sum(
        (group_of[:, None] == levels[None, :]).astype(jnp.float32) * calib_gain[None, :], axis=1
    )

    momenta = momentum_weights()
    forward_pairs = [(i, i + 1) for i in range(lines - 1)]
    backward_pairs = [(i + 1, i) for i in range(lines - 1)]

    earlier = previous_image.reshape(2, cl, rows, p_len, q_len)
    latest = current_image.reshape(2, cl, rows, p_len, q_len)

    def edge_blend(lo, hi):
        cur = latest[:, :, lo:hi]
        return cur + momenta[0] * (cur - earlier[:, :, lo:hi])

    low = lax.ppermute(edge_blend(rows - HALO, rows), "line", forward_pairs)
    high = lax.ppermute(edge_blend(0, HALO), "line", backward_pairs)

    table = jnp.stack([tap_index, range_offset])
    table = jnp.broadcast_to(table[None], (lines,) + table.shape)
    table = lax.all_to_all(table, "line", split_axis=0, concat_axis=2, tiled=True)[0]

    blended = latest + momenta[0] * (latest - earlier)

    local_taps = tap_table(tap_index, kernel_table)
    local_weights = shift_weights(range_offset, local_taps)
    angles = doppler_phase[None, :, :] + channel_ramp[:, None, :]
    cos_a = jnp.cos(angles)
    sin_a = jnp.sin(angles)
    gain = channel_gain[:, None, None]
    back_r = gain * (cos_a * observed[0] + sin_a * observed[1])
    back_i = gain * (cos_a * observed[1] - sin_a * observed[0])
    data = adjoint_shift(jnp.stack([back_r, back_i]), local_weights)
    data = data * (step_length / math.sqrt(na))
    data, low, high, table = lax.optimization_barrier((data, low, high, table))
    data = data.reshape(2, cl, data.shape[2], data.shape[3] // p_len, p_len)
    halves = 2 if cl % 2 == 0 else 1
    pieces = []
    for h in range(halves):
        piece = data[:, h * cl // halves : (h + 1) * cl // halves]
        if pieces:
            piece, pieces[-1] = lax.optimization_barrier((piece, pieces[-1]))
        pieces.append(lax.all_to_all(piece, "line", split_axis=2, concat_axis=3, tiled=True))
    taps = tap_table(table[0], kernel_table)
    weights = shift_weights(table[1], taps)

    def spectral(v):
        return v.reshape(v.shape[:-1] + (q_len, p_len)).swapaxes(-1, -2)

    weights = spectral(weights)
    band = [
        spectral(sum(taps[:, k] * taps[:, k + e] for k in range(K - e))) for e in range(K)
    ]
    coef = (channel_gain * channel_gain) * (step_length / na)

    first = (me == 0)
    last = (me == lines - 1)

    def wgt(d):
        return weights[d - LOWEST]

    undo = None
    for iteration in range(ITERS):
        if iteration > 0:
            blended = latest + momenta[iteration] * (latest - earlier)
            low = lax.ppermute(blended[:, :, rows - HALO :], "line", forward_pairs)
            high = lax.ppermute(blended[:, :, :HALO], "line", backward_pairs)
            if iteration == ITERS - 1:
                prior = latest.reshape(current_image.shape)
                low, high, prior = lax.optimization_barrier((low, high, prior))
        elif ITERS == 1:
            prior = current_image
        own = forward_transform(blended.reshape(2, -1, p_len, q_len), p_len, q_len)
        own = own.reshape(2, cl, rows, p_len, q_len)
        rim = jnp.concatenate([low, high], axis=2).reshape(2, -1, p_len, q_len)
        rim = forward_transform(rim, p_len, q_len)
        rim = rim.reshape(2, cl, 2 * HALO, p_len, q_len)

        def at(r):
            if r < HALO:
                return rim[:, :, r]
            if r < HALO + rows:
                return own[:, :, r - HALO]
            return rim[:, :, r - rows]

        gram = []
        for r in range(rows):
            c = r + HALO
            acc = band[0] * at(c)
            for e in range(1, K):
                acc = acc + band[e] * (at(c - e) + at(c + e))
            gram.append(acc)
        low_fix = []
        for rr in range(K):
            acc = None
            for s in range(1, K + 1):
                if rr + s > OFFMAX + K // 2:
                    continue
                u = None
                for j in range(K):
                    if j + s > OFFMAX + K // 2:
                        continue
                    term = wgt(j + s) * at(HALO + j)
                    u = term if u is None else u + term
                term = wgt(rr + s) * u
                acc = term if acc is None else acc + term
            low_fix.append(acc)
        high_fix = []
        for tt in range(-(K - 2), 1):
            acc = None
            for s in range(1, K):
                if tt - s < LOWEST:
                    continue
                u = None
                for t in range(-(K - 2), 1):
                    if t - s < LOWEST:
                        continue
                    term = wgt(t - s) * at(HALO + rows - 1 + t)
                    u = term if u is None else u + term
                term = wgt(tt - s) * u
                acc = term if acc is None else acc + term
            high_fix.append(acc)
        for rr in range(K):
            gram[rr] = gram[rr] - jnp.where(first, low_fix[rr], 0.0)
        for idx, tt in enumerate(range(-(K - 2), 1)):
            r = rows - 1 + tt
            gram[r] = gram[r] - jnp.where(last, high_fix[idx], 0.0)
        gram = jnp.stack(gram, axis=2)
        resid = coef[None, :, None, None, None] * gram
        grad = inverse_transform(resid.reshape(2, -1, p_len, q_len), p_len, q_len)
        if undo is None:
            undo = []
            for piece in pieces:
                part = swap_minor(piece.reshape(-1, q_len, p_len))
                part = inverse_transform(part.reshape(2, -1, p_len, q_len), p_len, q_len)
                undo.append(part.reshape(2, -1, rows, p_len, q_len))
            undo = jnp.concatenate(undo, axis=1)
        shifted = blended - grad.reshape(blended.shape) + undo
        squares = jnp.sum(shifted * shifted, axis=(0, 1))
        if chans == 2:
            squares = squares + lax.ppermute(squares, "chan", [(0, 1), (1, 0)])
        else:
            squares = lax.psum(squares, "chan")
        factor = shrink(squares)
        earlier = latest
        latest = shifted * factor[None, None]
    return (latest.reshape(current_image.shape), prior)


def solution(mesh):
    in_specs = (
        P(None, "chan", None, "line"),
        P(None, "chan", "line", None),
        P(None, "chan", "line", None),
        P(None, "line"),
        P("chan", "line"),
        P("line"),
        P("line"),
        P(),
        P("chan"),
        P(),
    )
    out_specs = (P(None, "chan", "line", None), P(None, "chan", "line", None))
    return jax.shard_map(body, mesh=mesh, in_specs=in_specs, out_specs=out_specs, check_vma=False)
```

```python
import math

import numpy as np
import jax
import jax.numpy as jnp
from jax import lax
from jax.sharding import PartitionSpec as P
from jax.experimental import pallas as pl

K = 4
Q = 16
OFFMAX = 2
G = 4
ITERS = 2
START_ITER = 8
HALO = K - 1

step_length = 0.25
threshold = 3.0


def momentum_weights():
    current = 1.0
    for counter in range(1, START_ITER):
        current = (1.0 + math.sqrt(1.0 + 4.0 * current * current)) / 2.0
    momenta = []
    for counter in range(ITERS):
        following = (1.0 + math.sqrt(1.0 + 4.0 * current * current)) / 2.0
        momenta.append((current - 1.0) / following)
        current = following
    return momenta


def tap_table(tap_index, kernel_table):
    levels = jnp.arange(Q, dtype=jnp.int32)
    onehot = (tap_index[:, None] == levels[None, :]).astype(jnp.float32)
    return jnp.dot(
        onehot, kernel_table, precision=lax.Precision.HIGHEST, preferred_element_type=jnp.float32
    )


def shift_weights(range_offset, tap_weights):
    stacked = []
    for displacement in range(-(OFFMAX + K // 2 - 1), OFFMAX + K // 2 + 1):
        summed = jnp.zeros(range_offset.shape, jnp.float32)
        for tap_number in range(K):
            matches = (range_offset + (tap_number - (K // 2 - 1)) == displacement).astype(
                jnp.float32
            )
            summed = summed + tap_weights[..., tap_number] * matches
        stacked.append(summed)
    return jnp.stack(stacked)


LOWEST = -(OFFMAX + K // 2 - 1)


def adjoint_shift(rows, weights):
    rim_width = OFFMAX + K // 2
    count = rows.shape[-2]
    pad = [(0, 0)] * rows.ndim
    pad[-2] = (rim_width, rim_width)
    padded = jnp.pad(rows, pad)
    summed = None
    for position in range(weights.shape[0]):
        displacement = LOWEST + position
        anchor = rim_width - displacement
        sliced = lax.slice_in_dim(padded, anchor, anchor + count, axis=rows.ndim - 2)
        weighted = sliced * weights[position]
        summed = weighted if summed is None else summed + weighted
    return summed


def left_block(count, sign):
    counter = np.arange(count)
    angle = (np.outer(counter, counter) % count) * (2.0 * np.pi / count)
    c = np.cos(angle)
    s = sign * np.sin(angle)
    return jnp.asarray(np.block([[c, -s], [s, c]]), jnp.float32)


def right_block(count, sign):
    counter = np.arange(count)
    angle = (np.outer(counter, counter) % count) * (2.0 * np.pi / count)
    c = np.cos(angle)
    s = sign * np.sin(angle)
    return jnp.asarray(np.block([[c, s], [-s, c]]), jnp.float32)


def twiddle(rows, cols, total, sign):
    angle = (np.outer(np.arange(rows), np.arange(cols)) % total) * (2.0 * np.pi / total)
    return jnp.asarray(np.stack([np.cos(angle), sign * np.sin(angle)]), jnp.float32)


def dot(a, b):
    return jnp.dot(a, b, precision=lax.Precision.HIGH, preferred_element_type=jnp.float32)


def forward_kernel(x_ref, w_ref, v_ref, t_ref, o_ref):
    nb, p_len, q_len = x_ref.shape[1], x_ref.shape[2], x_ref.shape[3]
    stacked = jnp.concatenate(
        [
            jnp.concatenate([x_ref[0, b] for b in range(nb)], axis=1),
            jnp.concatenate([x_ref[1, b] for b in range(nb)], axis=1),
        ],
        axis=0,
    )
    mid = dot(w_ref[...], stacked)
    tc = jnp.concatenate([t_ref[0]] * nb, axis=1)
    ts = jnp.concatenate([t_ref[1]] * nb, axis=1)
    mr = mid[:p_len]
    mi = mid[p_len:]
    tr = mr * tc - mi * ts
    ti = mi * tc + mr * ts
    turned = jnp.concatenate(
        [
            jnp.concatenate([tr[:, b * q_len : (b + 1) * q_len], ti[:, b * q_len : (b + 1) * q_len]], axis=1)
            for b in range(nb)
        ],
        axis=0,
    )
    out = dot(turned, v_ref[...])
    for b in range(nb):
        o_ref[0, b] = out[b * p_len : (b + 1) * p_len, :q_len]
        o_ref[1, b] = out[b * p_len : (b + 1) * p_len, q_len:]


def inverse_kernel(y_ref, v_ref, w_ref, t_ref, o_ref):
    nb, p_len, q_len = y_ref.shape[1], y_ref.shape[2], y_ref.shape[3]
    stacked = jnp.concatenate(
        [jnp.concatenate([y_ref[0, b], y_ref[1, b]], axis=1) for b in range(nb)], axis=0
    )
    mid = dot(stacked, v_ref[...])
    tc = jnp.concatenate([t_ref[0]] * nb, axis=0)
    ts = jnp.concatenate([t_ref[1]] * nb, axis=0)
    mr = mid[:, :q_len]
    mi = mid[:, q_len:]
    tr = mr * tc - mi * ts
    ti = mi * tc + mr * ts
    turned = jnp.concatenate(
        [
            jnp.concatenate([tr[b * p_len : (b + 1) * p_len] for b in range(nb)], axis=1),
            jnp.concatenate([ti[b * p_len : (b + 1) * p_len] for b in range(nb)], axis=1),
        ],
        axis=0,
    )
    out = dot(w_ref[...], turned)
    for b in range(nb):
        o_ref[0, b] = out[:p_len, b * q_len : (b + 1) * q_len]
        o_ref[1, b] = out[p_len:, b * q_len : (b + 1) * q_len]


def transpose_kernel(x_ref, o_ref):
    for b in range(x_ref.shape[0]):
        o_ref[b] = x_ref[b].T


def swap_minor(x):
    total, p_len, q_len = x.shape
    nb = block_count(total)
    return pl.pallas_call(
        transpose_kernel,
        out_shape=jax.ShapeDtypeStruct((total, q_len, p_len), x.dtype),
        grid=(total // nb,),
        in_specs=[pl.BlockSpec((nb, p_len, q_len), lambda i: (i, 0, 0))],
        out_specs=pl.BlockSpec((nb, q_len, p_len), lambda i: (i, 0, 0)),
        cost_estimate=pl.CostEstimate(flops=0, bytes_accessed=2 * x.size * 4, transcendentals=0),
    )(x)


def block_count(total):
    for nb in (32, 16, 8, 7, 6, 5, 4, 3, 2, 1):
        if total % nb == 0:
            return nb
    return 1


def run_transform(kernel, data, first, second, turn):
    _, total, p_len, q_len = data.shape
    nb = block_count(total)
    flops = 2 * 2 * total * (2 * p_len) * (2 * q_len) * (p_len + q_len) // 2
    return pl.pallas_call(
        kernel,
        out_shape=jax.ShapeDtypeStruct(data.shape, jnp.float32),
        grid=(total // nb,),
        in_specs=[
            pl.BlockSpec((2, nb, p_len, q_len), lambda i: (0, i, 0, 0)),
            pl.BlockSpec(first.shape, lambda i: (0, 0)),
            pl.BlockSpec(second.shape, lambda i: (0, 0)),
            pl.BlockSpec(turn.shape, lambda i: (0, 0, 0)),
        ],
        out_specs=pl.BlockSpec((2, nb, p_len, q_len), lambda i: (0, i, 0, 0)),
        cost_estimate=pl.CostEstimate(
            flops=flops, bytes_accessed=2 * data.size * 4, transcendentals=0
        ),
    )(data, first, second, turn)


def forward_transform(x, p_len, q_len):
    return run_transform(
        forward_kernel,
        x,
        left_block(p_len, -1.0),
        right_block(q_len, -1.0),
        twiddle(p_len, q_len, p_len * q_len, -1.0),
    )


def inverse_transform(y, p_len, q_len):
    return run_transform(
        inverse_kernel,
        y,
        right_block(q_len, 1.0),
        left_block(p_len, 1.0),
        twiddle(p_len, q_len, p_len * q_len, 1.0),
    )


def shrink(squares):
    magnitude = jnp.sqrt(squares)
    return jnp.maximum(magnitude - threshold, 0.0) / jnp.maximum(magnitude, threshold)


def body(
    observed,
    current_image,
    previous_image,
    doppler_phase,
    channel_ramp,
    range_offset,
    tap_index,
    kernel_table,
    group_of,
    calib_gain,
):
    lines = lax.axis_size("line")
    chans = lax.axis_size("chan")
    me = lax.axis_index("line")
    _, cl, rows, na = current_image.shape
    p_len = 128 if na % 128 == 0 else 1
    q_len = na // p_len

    levels = jnp.arange(G, dtype=jnp.int32)
    channel_gain = jnp.sum(
        (group_of[:, None] == levels[None, :]).astype(jnp.float32) * calib_gain[None, :], axis=1
    )

    momenta = momentum_weights()
    forward_pairs = [(i, i + 1) for i in range(lines - 1)]
    backward_pairs = [(i + 1, i) for i in range(lines - 1)]

    earlier = previous_image.reshape(2, cl, rows, p_len, q_len)
    latest = current_image.reshape(2, cl, rows, p_len, q_len)

    def edge_blend(lo, hi):
        cur = latest[:, :, lo:hi]
        return cur + momenta[0] * (cur - earlier[:, :, lo:hi])

    low = lax.ppermute(edge_blend(rows - HALO, rows), "line", forward_pairs)
    high = lax.ppermute(edge_blend(0, HALO), "line", backward_pairs)

    table = jnp.stack([tap_index, range_offset])
    table = jnp.broadcast_to(table[None], (lines,) + table.shape)
    table = lax.all_to_all(table, "line", split_axis=0, concat_axis=2, tiled=True)[0]

    blended = latest + momenta[0] * (latest - earlier)

    local_taps = tap_table(tap_index, kernel_table)
    local_weights = shift_weights(range_offset, local_taps)
    angles = doppler_phase[None, :, :] + channel_ramp[:, None, :]
    cos_a = jnp.cos(angles)
    sin_a = jnp.sin(angles)
    gain = channel_gain[:, None, None]
    back_r = gain * (cos_a * observed[0] + sin_a * observed[1])
    back_i = gain * (cos_a * observed[1] - sin_a * observed[0])
    data = adjoint_shift(jnp.stack([back_r, back_i]), local_weights)
    data = data * (step_length / math.sqrt(na))
    data, low, high, table = lax.optimization_barrier((data, low, high, table))
    data = data.reshape(2, cl, data.shape[2], data.shape[3] // p_len, p_len)
    halves = 2 if cl % 2 == 0 else 1
    pieces = []
    for h in range(halves):
        piece = data[:, h * cl // halves : (h + 1) * cl // halves]
        if pieces:
            piece, pieces[-1] = lax.optimization_barrier((piece, pieces[-1]))
        pieces.append(lax.all_to_all(piece, "line", split_axis=2, concat_axis=3, tiled=True))
    taps = tap_table(table[0], kernel_table)
    weights = shift_weights(table[1], taps)

    def spectral(v):
        return v.reshape(v.shape[:-1] + (q_len, p_len)).swapaxes(-1, -2)

    weights = spectral(weights)
    band = [
        spectral(sum(taps[:, k] * taps[:, k + e] for k in range(K - e))) for e in range(K)
    ]
    coef = (channel_gain * channel_gain) * (step_length / na)

    first = (me == 0)
    last = (me == lines - 1)

    def wgt(d):
        return weights[d - LOWEST]

    undo = None
    for iteration in range(ITERS):
        if iteration > 0:
            blended = latest + momenta[iteration] * (latest - earlier)
            low = lax.ppermute(blended[:, :, rows - HALO :], "line", forward_pairs)
            high = lax.ppermute(blended[:, :, :HALO], "line", backward_pairs)
            if iteration == ITERS - 1:
                prior = latest.reshape(current_image.shape)
                low, high, prior = lax.optimization_barrier((low, high, prior))
        elif ITERS == 1:
            prior = current_image
        own = forward_transform(blended.reshape(2, -1, p_len, q_len), p_len, q_len)
        own = own.reshape(2, cl, rows, p_len, q_len)
        rim = jnp.concatenate([low, high], axis=2).reshape(2, -1, p_len, q_len)
        rim = forward_transform(rim, p_len, q_len)
        rim = rim.reshape(2, cl, 2 * HALO, p_len, q_len)

        def at(r):
            if r < HALO:
                return rim[:, :, r]
            if r < HALO + rows:
                return own[:, :, r - HALO]
            return rim[:, :, r - rows]

        gram = []
        for r in range(rows):
            c = r + HALO
            acc = band[0] * at(c)
            for e in range(1, K):
                acc = acc + band[e] * (at(c - e) + at(c + e))
            gram.append(acc)
        low_fix = []
        for rr in range(K):
            acc = None
            for s in range(1, K + 1):
                if rr + s > OFFMAX + K // 2:
                    continue
                u = None
                for j in range(K):
                    if j + s > OFFMAX + K // 2:
                        continue
                    term = wgt(j + s) * at(HALO + j)
                    u = term if u is None else u + term
                term = wgt(rr + s) * u
                acc = term if acc is None else acc + term
            low_fix.append(acc)
        high_fix = []
        for tt in range(-(K - 2), 1):
            acc = None
            for s in range(1, K):
                if tt - s < LOWEST:
                    continue
                u = None
                for t in range(-(K - 2), 1):
                    if t - s < LOWEST:
                        continue
                    term = wgt(t - s) * at(HALO + rows - 1 + t)
                    u = term if u is None else u + term
                term = wgt(tt - s) * u
                acc = term if acc is None else acc + term
            high_fix.append(acc)
        for rr in range(K):
            gram[rr] = gram[rr] - jnp.where(first, low_fix[rr], 0.0)
        for idx, tt in enumerate(range(-(K - 2), 1)):
            r = rows - 1 + tt
            gram[r] = gram[r] - jnp.where(last, high_fix[idx], 0.0)
        gram = jnp.stack(gram, axis=2)
        resid = coef[None, :, None, None, None] * gram
        grad = inverse_transform(resid.reshape(2, -1, p_len, q_len), p_len, q_len)
        if undo is None:
            undo = []
            for piece in pieces:
                part = swap_minor(piece.reshape(-1, q_len, p_len))
                part = inverse_transform(part.reshape(2, -1, p_len, q_len), p_len, q_len)
                undo.append(part.reshape(2, -1, rows, p_len, q_len))
            undo = jnp.concatenate(undo, axis=1)
        shifted = blended - grad.reshape(blended.shape) + undo
        squares = jnp.sum(shifted * shifted, axis=(0, 1))
        if chans == 2:
            squares = squares + lax.ppermute(squares, "chan", [(0, 1), (1, 0)])
        else:
            squares = lax.psum(squares, "chan")
        factor = shrink(squares)
        earlier = latest
        latest = shifted * factor[None, None]
    return (latest.reshape(current_image.shape), prior)


def solution(mesh):
    in_specs = (
        P(None, "chan", None, "line"),
        P(None, "chan", "line", None),
        P(None, "chan", "line", None),
        P(None, "line"),
        P("chan", "line"),
        P("line"),
        P("line"),
        P(),
        P("chan"),
        P(),
    )
    out_specs = (P(None, "chan", "line", None), P(None, "chan", "line", None))
    return jax.shard_map(body, mesh=mesh, in_specs=in_specs, out_specs=out_specs, check_vma=False)
```
